512 devices in a mesh: ctx: 128 (over y, z, core), tp: 4 (over x).
Axes of the slice: x: 4, y: 8, z: 8, core: 2. Of those that a mesh axis runs over, the one named last changes fastest.
Arguments:
- hidden_in: bfloat16 [16384, 1536], P('ctx', 'tp'), may hold values from -60 to 60
- queries: bfloat16 [16384, 2048], P('ctx', 'tp'), may hold values from -200 to 200
- rotated_key_value: bfloat16 [16384, 4, 128], P('ctx', 'tp'), may hold values from -5 to 5
- sink_logit_table: float32 [32], P('tp'), may hold values from -2 to 2
- out_proj: bfloat16 [2048, 1536], P('tp', 'ctx'), may hold values from -0.125 to 0.125
- norm_gain: float32 [1536], P('tp'), may hold values from 0.1 to 1.9
- expert_in: bfloat16 [128, 2, 1536, 1536], P('ctx', None, None, 'tp'), may hold values from -0.15625 to 0.15625
- expert_out: bfloat16 [128, 1536, 1536], P('ctx', 'tp'), may hold values from -0.15625 to 0.15625
- routes: int32 [16384, 4], P('ctx'), may hold values from 0 to 127, all different within a row; in each aligned block of 128 rows (0 to 127, 128 to 255, ...) at most 12 rows name the same one
- route_scores: float32 [16384, 4], P('ctx'), may hold values from 0.05 to 1
Outputs:
- layer_out: bfloat16 [16384, 1536], P('ctx', 'tp')
The draws below stay inside these ranges and needn't reach their ends.
Inputs may be any that keep to these rules, and one draw needn't show every extreme that they name: `routes`: each token names 4 different experts. In every aligned block of 128 tokens (the tokens of one device) no expert is named by more than 12 tokens, a bound that some block reaches.
All inputs are finite; a program needn't handle non-finite values.
Results may differ from the reference program's by a relative error of at most 0.008.
Values may be sent and summed in bfloat16 or wider, within the bound.
No kernel may reach another device: no remote copies, remote signals or barrier semaphores. Data moves between devices by JAX's collectives and lax.ppermute only.
A program may use at most 64 MiB of HBM per device.

```python
import math
import jax
import jax.numpy as jnp
import numpy as np
from jax import lax

D = 1536
FF = 1536
QUERY_HEADS = 32
KEY_VALUE_HEADS = 4
HEAD_SIZE = 64
TOP = 4
WINDOW_KEYS = 128
TOK_DEV = 128
EXPERTS = 128
TOKEN_TOTAL = 16384
CAP = 12
N_CTX = 128
N_TP = 4


def attention_base(key):
    query_key = jax.random.fold_in(key, 101)
    paired_key = jax.random.fold_in(key, 102)
    query_matrix = jnp.clip(jax.random.normal(query_key, (TOKEN_TOTAL, QUERY_HEADS, HEAD_SIZE), jnp.float32), -5.0, 5.0)
    paired_value = jnp.clip(jax.random.normal(paired_key, (TOKEN_TOTAL, KEY_VALUE_HEADS, 2, HEAD_SIZE), jnp.float32), -5.0, 5.0)
    return (query_matrix.reshape(TOKEN_TOTAL, QUERY_HEADS * HEAD_SIZE), paired_value.reshape(TOKEN_TOTAL, KEY_VALUE_HEADS, 2 * HEAD_SIZE))


def draw_queries(key, part):
    return attention_base(key)[0].astype(jnp.bfloat16)


def draw_rotated_key_value(key, part):
    return attention_base(key)[1].astype(jnp.bfloat16)


def draw_hidden_in(key, part):
    noise_key = jax.random.fold_in(key, 201)
    column_key = jax.random.fold_in(key, 202)
    row_key = jax.random.fold_in(key, 203)
    noise = jnp.clip(jax.random.normal(noise_key, (TOKEN_TOTAL, D), jnp.float32), -5.0, 5.0)
    ramp = 3.0 ** (jnp.arange(D, dtype=jnp.float32) / D - 0.5)
    columns = jnp.exp(jax.random.uniform(column_key, (D,), jnp.float32, math.log(0.3), math.log(3.0))) * ramp
    row_scale = jnp.exp(jax.random.uniform(row_key, (TOKEN_TOTAL, 1), jnp.float32, math.log(0.5), math.log(2.0)))
    values = noise * columns * row_scale
    return values.astype(jnp.bfloat16)


def block_scale(own_key, dims, split, least, top_value):
    level, own = 1.0, jax.random.fold_in(own_key, 6)
    for axis_at, shards_of in split:
        steps = jnp.exp(jax.random.uniform(jax.random.fold_in(own, axis_at), (shards_of,), jnp.float32, least / len(split), top_value / len(split)))
        level = level * jnp.repeat(steps, dims[axis_at] // shards_of).reshape([-1 if axis == axis_at else 1 for axis in range(len(dims))])
    return level


def shared_out(own_key, own, number, rows, count, top, reach, lean):
    order = jax.random.permutation(own_key, count)
    packed, ordinary = portions_of(count, rows * top, reach, lean, True), portions_of(count, rows * top, reach, lean, False)
    places = jnp.arange(count)

    def named(lengths, rotation):
        used = int((lengths > 0).sum())
        fixed = max(1, used // 4)
        moved = fixed + (places - fixed + rotation * (used - fixed)) % max(1, count - fixed)
        return jnp.zeros((count,), jnp.int32).at[order[jnp.where(places < fixed, places, moved)]].set(jnp.asarray(lengths, jnp.int32))

    lengths = jnp.where(number % 4 == 0, named(packed, number // 4), named(ordinary, number - number // 4 - 1))
    mixed = jax.random.permutation(jax.random.fold_in(own, 3), count)
    giver, taker = mixed[0:count // 2 * 2:2], mixed[1:count // 2 * 2:2]
    margin = jnp.minimum(lengths[giver] - 1, reach - lengths[taker]) // 2
    margin = jnp.where((giver == order[0]) | (taker == order[0]) | (lengths[taker] == 0), 0, jnp.maximum(margin, 0))
    moved = jax.random.randint(jax.random.fold_in(own, 4), (count // 2,), 0, 1 << 20) % (margin + 1)
    lengths = lengths.at[giver].add(-moved).at[taker].add(moved)
    members = jnp.searchsorted(jnp.cumsum(lengths), jnp.arange(rows * top), side="right").astype(jnp.int32)
    grid = members.reshape(top, rows).T
    grid = grid[jax.random.permutation(jax.random.fold_in(own, 1), rows)]
    rotation = jax.random.randint(jax.random.fold_in(own, 2), (rows, 1), 0, top)
    return jnp.take_along_axis(grid, (jnp.arange(top)[None, :] + rotation) % top, axis=1)


def portions_of(number_of, total, bound, slope, full):
    weights = [(1 << 20) // math.isqrt(standing ** slope) + 1 for standing in range(1, number_of + 1)]
    largest = bound if full else min(bound, max(-(-total // number_of), total * weights[0] // sum(weights)))
    least = 1 if total - largest >= number_of - 1 else 0
    holding, rest = [largest] + [least] * (number_of - 1), total - largest - least * (number_of - 1)
    while rest > 0:
        movable = [i for i in range(1, number_of) if holding[i] < largest] or [i for i in range(1, number_of) if holding[i] < bound]
        mass, budget = sum([weights[i] for i in movable]), rest
        for i in movable:
            more = min(bound - holding[i], max(1, budget * weights[i] // mass), rest)
            holding[i] = holding[i] + more
            rest = rest - more
    return np.array(holding)


def scatter_about(own_key, shape, scale, most, pieces=(), kind=jnp.bfloat16):
    level = block_scale(own_key, shape, pieces, -0.22, 0.18) if pieces else 1.0
    entries = jax.random.normal(own_key, shape, jnp.float32) * scale * level
    return jnp.minimum(jnp.maximum(entries, -most), most).astype(kind)


def setup_inputs(seed: int = 0) -> dict:
    seeds = jax.random.split(jax.random.key(seed), 11)
    hidden_in = draw_hidden_in(jax.random.fold_in(seeds[10], 71), 0)
    queries = draw_queries(jax.random.fold_in(seeds[10], 71), 0)
    rotated_key_value = draw_rotated_key_value(jax.random.fold_in(seeds[10], 71), 0)
    sink_logit_table = jnp.clip(jax.random.uniform(seeds[3], (QUERY_HEADS,), jnp.float32, -2.0, 2.0) * block_scale(seeds[3], (QUERY_HEADS,), ((0, 4),), -0.4, 0.0), -2.0, 2.0)
    out_proj = scatter_about(seeds[4], (QUERY_HEADS * HEAD_SIZE, D), (QUERY_HEADS * HEAD_SIZE) ** -0.5, 0.125, ((0, 4), (1, 128)))
    norm_gain = jnp.clip(1.0 + 0.18 * jax.random.normal(seeds[5], (D,), jnp.float32), 0.1, 1.9)
    expert_in = scatter_about(seeds[6], (EXPERTS, 2, D, FF), D ** -0.5, 0.15625, ((0, 128), (3, 4)))
    expert_out = scatter_about(seeds[7], (EXPERTS, FF, D), FF ** -0.5, 0.15625, ((0, 128), (1, 4)))
    routes_keys = jax.random.split(jax.random.fold_in(seeds[8], 1), TOKEN_TOTAL // TOK_DEV)
    routes_turns = jax.random.permutation(jax.random.fold_in(seeds[8], 3), TOKEN_TOTAL // TOK_DEV)
    routes = jax.vmap(lambda own, number: shared_out(jax.random.fold_in(seeds[8], 2), own, number, TOK_DEV, EXPERTS, TOP, CAP, 2))(routes_keys, routes_turns).reshape((TOKEN_TOTAL, TOP))
    route_scores = jnp.clip(jnp.exp(math.log(1.0) - 2.9957323 * jax.random.uniform(seeds[9], (TOKEN_TOTAL, TOP), jnp.float32) ** block_scale(seeds[9], (TOKEN_TOTAL, TOP), ((0, 128),), -0.2, 0.2)), 0.05, 1.0)
    return dict(hidden_in=hidden_in, queries=queries, rotated_key_value=rotated_key_value, sink_logit_table=sink_logit_table, out_proj=out_proj, norm_gain=norm_gain, expert_in=expert_in, expert_out=expert_out, routes=routes, route_scores=route_scores)


def attend(query_block, key_blk, value_blk, inside, sink_row_block, factor):
    score = jnp.einsum('rgqd,sgd->gqrs', query_block.astype(jnp.float32), key_blk.astype(jnp.float32)) * factor
    masked = jnp.where(inside, score, -1e+30)
    top_score = jnp.maximum(lax.optimization_barrier(jnp.max(masked, -1)), sink_row_block[:, :, None])
    expvals = jnp.where(inside, jnp.exp(score - top_score[..., None]), 0.0)
    denominator = lax.optimization_barrier(jnp.sum(expvals, -1)) + jnp.exp(sink_row_block[:, :, None] - top_score)
    probs = (expvals / denominator[..., None]).astype(jnp.bfloat16)
    mixed = jnp.einsum('gqrs,sgd->rgqd', probs.astype(jnp.float32), value_blk.astype(jnp.float32))
    return mixed.astype(jnp.bfloat16)

def reference(hidden_in, queries, rotated_key_value, sink_logit_table, out_proj, norm_gain, expert_in, expert_out, routes, route_scores):
    factor = HEAD_SIZE ** (-0.5)
    queries_per_group = QUERY_HEADS // KEY_VALUE_HEADS
    block_row_count = TOK_DEV * math.gcd(N_CTX, max(1, 512 // TOK_DEV))
    key_value_padding = jnp.concatenate([jnp.zeros((WINDOW_KEYS, KEY_VALUE_HEADS, 2 * HEAD_SIZE), jnp.bfloat16), rotated_key_value], 0)
    sink_row_block = sink_logit_table.reshape(KEY_VALUE_HEADS, queries_per_group)

    def attend_block(block_id):
        start_shift = block_id * block_row_count
        query_block = lax.dynamic_slice_in_dim(queries, start_shift, block_row_count, 0).reshape(block_row_count, KEY_VALUE_HEADS, queries_per_group, HEAD_SIZE)
        kv_blk = lax.dynamic_slice_in_dim(key_value_padding, start_shift, block_row_count + WINDOW_KEYS, 0)
        query_pos = start_shift + jnp.arange(block_row_count, dtype=jnp.int32)[:, None]
        key_pos = start_shift - WINDOW_KEYS + jnp.arange(block_row_count + WINDOW_KEYS, dtype=jnp.int32)[None, :]
        inside = (key_pos <= query_pos) & (key_pos > query_pos - WINDOW_KEYS) & (key_pos >= 0)
        mixed = attend(query_block, kv_blk[..., :HEAD_SIZE], kv_blk[..., HEAD_SIZE:], inside, sink_row_block, factor)
        return mixed.reshape(block_row_count, QUERY_HEADS * HEAD_SIZE)
    attended = lax.map(attend_block, jnp.arange(TOKEN_TOTAL // block_row_count, dtype=jnp.int32)).reshape(TOKEN_TOTAL, QUERY_HEADS * HEAD_SIZE)
    residual = hidden_in.astype(jnp.float32) + jnp.dot(attended, out_proj, preferred_element_type=jnp.float32)
    mean_sq = lax.optimization_barrier(jnp.mean(residual * residual, -1, keepdims=True))
    normed = (residual * lax.rsqrt(mean_sq + 1e-05) * norm_gain).astype(jnp.bfloat16)
    local_routes = routes.reshape(N_CTX, TOK_DEV, TOP)
    expert_ids = jnp.arange(EXPERTS, dtype=jnp.int32)
    onehot = (local_routes[..., None] == expert_ids).astype(jnp.int32)
    per_tok = lax.optimization_barrier(jnp.sum(onehot, 2))
    before = jnp.cumsum(per_tok, axis=1) - per_tok
    slot_ids = lax.optimization_barrier(jnp.sum(onehot * before[:, :, None, :], -1))
    weights = (route_scores / lax.optimization_barrier(jnp.sum(route_scores, -1, keepdims=True))).reshape(N_CTX, TOK_DEV, TOP)
    source_ids = jnp.broadcast_to(jnp.arange(N_CTX, dtype=jnp.int32)[:, None, None], local_routes.shape)
    token_ids = jnp.broadcast_to(jnp.arange(TOK_DEV, dtype=jnp.int32)[None, :, None], local_routes.shape)
    slot_table = jnp.full((EXPERTS, N_CTX, CAP), TOK_DEV, jnp.int32).at[local_routes, source_ids, slot_ids].set(token_ids)
    slot_weights = jnp.zeros((EXPERTS, N_CTX, CAP), jnp.float32).at[local_routes, source_ids, slot_ids].set(weights)
    normed_pad = jnp.concatenate([normed.reshape(N_CTX, TOK_DEV, D), jnp.zeros((N_CTX, 1, D), jnp.bfloat16)], 1)
    source_rows = jnp.arange(N_CTX, dtype=jnp.int32)[:, None]
    quarter = FF // N_TP

    def expert(running, expert_data):
        table, slot_w, w_in, w_out = expert_data
        row_data = normed_pad[source_rows, table].reshape(N_CTX * CAP, D)
        summed = jnp.zeros((N_CTX * CAP, D), jnp.float32)
        for quarter_id in range(N_TP):
            lower = quarter_id * quarter
            gate_vals = jnp.dot(row_data, w_in[0, :, lower:lower + quarter], preferred_element_type=jnp.float32)
            up_vals = jnp.dot(row_data, w_in[1, :, lower:lower + quarter], preferred_element_type=jnp.float32)
            activated = ((up_vals + 1.0) * gate_vals * jax.nn.sigmoid(1.702 * gate_vals)).astype(jnp.bfloat16)
            partial_value = jnp.dot(activated, w_out[lower:lower + quarter], preferred_element_type=jnp.float32).astype(jnp.bfloat16)
            partial_value = lax.optimization_barrier(partial_value)
            summed = summed + partial_value.astype(jnp.float32)
        result = summed.astype(jnp.bfloat16)
        result = lax.optimization_barrier(result).reshape(N_CTX, CAP, D)
        running = running.at[source_rows, table].add(slot_w[..., None] * result.astype(jnp.float32))
        return (running, None)
    running, _ = lax.scan(expert, jnp.zeros((N_CTX, TOK_DEV + 1, D), jnp.float32), (slot_table, slot_weights, expert_in, expert_out))
    moe_sum = running[:, :TOK_DEV].reshape(TOKEN_TOTAL, D)
    return (residual + moe_sum).astype(jnp.bfloat16)
```

```python
import jax
import jax.numpy as jnp
from jax import lax
from jax.sharding import PartitionSpec as P

WINDOW_KEYS = 128


def shifted(value, axis, steps):
    count = lax.axis_size(axis)
    first, last = (max(0, -steps), min(count, count - steps))
    return lax.ppermute(value, axis, [(source, source + steps) for source in range(first, last)])


def attend(query_block, key_blk, value_blk, inside, sink_row_block, factor):
    score = (
        jnp.einsum("rgqd,sgd->gqrs", query_block, key_blk, preferred_element_type=jnp.float32)
        * factor
    )
    masked = jnp.where(inside, score, -1e30)
    top_score = jnp.maximum(jnp.max(masked, -1), sink_row_block[:, :, None])
    expvals = jnp.where(inside, jnp.exp(score - top_score[..., None]), 0.0)
    denominator = jnp.sum(expvals, -1) + jnp.exp(sink_row_block[:, :, None] - top_score)
    probs = (expvals / denominator[..., None]).astype(jnp.bfloat16)
    mixed = jnp.einsum("gqrs,sgd->rgqd", probs, value_blk, preferred_element_type=jnp.float32)
    return mixed.astype(jnp.bfloat16)


def body(
    hidden_in,
    queries,
    rotated_key_value,
    sink_logit_table,
    out_proj,
    norm_gain,
    expert_in,
    expert_out,
    routes,
    route_scores,
):
    tok_rows = hidden_in.shape[0]
    kv_heads = rotated_key_value.shape[1]
    head_dim = rotated_key_value.shape[2] // 2
    q_heads = sink_logit_table.shape[0]
    queries_per_group = q_heads // kv_heads
    factor = head_dim ** (-0.5)
    sink_row_block = sink_logit_table.reshape(kv_heads, queries_per_group)
    earlier = shifted(rotated_key_value, "ctx", 1)
    keys_all = jnp.concatenate([earlier, rotated_key_value], 0)
    first_pos = lax.axis_index("ctx") * tok_rows
    block_row_count = min(512, tok_rows)
    query_block = queries.reshape(block_row_count, kv_heads, queries_per_group, head_dim)
    query_pos = first_pos + 0 + jnp.arange(block_row_count, dtype=jnp.int32)[:, None]
    key_pos = (
        first_pos
        + 0
        - WINDOW_KEYS
        + jnp.arange(block_row_count + WINDOW_KEYS, dtype=jnp.int32)[None, :]
    )
    inside = (key_pos <= query_pos) & (key_pos > query_pos - WINDOW_KEYS) & (key_pos >= 0)
    mixed = attend(
        query_block,
        keys_all[..., :head_dim],
        keys_all[..., head_dim:],
        inside,
        sink_row_block,
        factor,
    )
    outputs = mixed.reshape(block_row_count, q_heads * head_dim)
    head_partial = jnp.dot(
        outputs,
        lax.all_gather(out_proj, "ctx", axis=1, tiled=True),
        preferred_element_type=jnp.float32,
    )
    d_model = head_partial.shape[1]
    residual = hidden_in.astype(jnp.float32) + lax.psum_scatter(
        head_partial.astype(jnp.bfloat16), "tp", scatter_dimension=1, tiled=True
    ).astype(jnp.float32)
    square_total = lax.psum(jnp.sum(residual * residual, -1), "tp")
    normed = (residual * lax.rsqrt(square_total[:, None] / d_model + 1e-05) * norm_gain).astype(
        jnp.bfloat16
    )
    ctx_count = lax.axis_size("ctx")
    tp_count = lax.axis_size("tp")
    top_count = routes.shape[1]
    experts = ctx_count * expert_in.shape[0]
    capacity = max(2, min(tok_rows, 3 * top_count * tok_rows // experts))
    quarter_w = d_model // tp_count
    onehot = (routes[:, :, None] == jnp.arange(experts, dtype=jnp.int32)).astype(jnp.int32)
    per_tok = jnp.sum(onehot, 1)
    before = jnp.cumsum(per_tok, axis=0) - per_tok
    slot_ids = jnp.sum(onehot * before[:, None, :], -1)
    flat_index = (routes * capacity + slot_ids).reshape(-1)
    weights = route_scores / jnp.sum(route_scores, -1, keepdims=True)
    tp_index = lax.axis_index("tp")
    spread = jnp.broadcast_to(normed[:, None, :], (tok_rows, top_count, quarter_w)).reshape(
        -1, quarter_w
    )
    outbox = jnp.zeros((experts * capacity, quarter_w), jnp.bfloat16).at[flat_index].set(spread)
    arrived = lax.all_to_all(
        outbox.reshape(ctx_count, capacity, quarter_w), "ctx", 0, 0, tiled=True
    ).reshape(-1, quarter_w)
    pieces = [arrived]
    for step in range(1, tp_count):
        pieces.append(lax.ppermute(arrived, "tp", [(i, (i + step) % tp_count) for i in range(tp_count)]))
    row_data = jnp.concatenate(pieces, 1)
    order = (tp_index - jnp.arange(tp_count, dtype=jnp.int32)) % tp_count
    hidden_w = expert_in.shape[3]
    w_gate = jnp.take(expert_in[0, 0].reshape(tp_count, quarter_w, hidden_w), order, axis=0).reshape(d_model, hidden_w)
    w_up = jnp.take(expert_in[0, 1].reshape(tp_count, quarter_w, hidden_w), order, axis=0).reshape(d_model, hidden_w)
    gate_vals = jnp.dot(row_data, w_gate, preferred_element_type=jnp.float32)
    up_vals = jnp.dot(row_data, w_up, preferred_element_type=jnp.float32)
    activated = ((up_vals + 1.0) * gate_vals * jax.nn.sigmoid(1.702 * gate_vals)).astype(
        jnp.bfloat16
    )
    def partial_for(quarter_id):
        cols = lax.dynamic_slice_in_dim(expert_out[0], quarter_id * quarter_w, quarter_w, 1)
        return jnp.dot(activated, cols, preferred_element_type=jnp.float32).astype(jnp.bfloat16)

    summed = partial_for(tp_index).astype(jnp.float32)
    for step in range(1, tp_count):
        piece = partial_for((tp_index + step) % tp_count)
        summed = summed + lax.ppermute(
            piece, "tp", [(i, (i + step) % tp_count) for i in range(tp_count)]
        ).astype(jnp.float32)
    result = summed.astype(jnp.bfloat16).reshape(ctx_count, capacity, quarter_w)
    returned = lax.all_to_all(result, "ctx", 0, 0, tiled=True).reshape(-1, quarter_w)
    expert_result = returned[flat_index].reshape(tok_rows, top_count, quarter_w)
    moe_sum = jnp.zeros((tok_rows, quarter_w), jnp.float32)
    for member in range(top_count):
        moe_sum = moe_sum + weights[:, member : member + 1] * expert_result[:, member].astype(
            jnp.float32
        )
    return (residual + moe_sum).astype(jnp.bfloat16)


def solution(mesh):
    in_specs = (
        P("ctx", "tp"),
        P("ctx", "tp"),
        P("ctx", "tp", None),
        P("tp"),
        P("tp", "ctx"),
        P("tp"),
        P("ctx", None, None, "tp"),
        P("ctx", "tp", None),
        P("ctx", None),
        P("ctx", None),
    )
    out_specs = P("ctx", "tp")
    return jax.shard_map(body, mesh=mesh, in_specs=in_specs, out_specs=out_specs, check_vma=False)
```

```python
import jax
import jax.numpy as jnp
from jax import lax
from jax.sharding import PartitionSpec as P

WINDOW_KEYS = 128


def shifted(value, axis, steps):
    count = lax.axis_size(axis)
    first, last = (max(0, -steps), min(count, count - steps))
    return lax.ppermute(value, axis, [(source, source + steps) for source in range(first, last)])


def gathered_columns(block):
    count = lax.axis_size("ctx")
    bits = count.bit_length() - 1
    me = lax.axis_index("ctx")
    order = []
    half = (bits - 1) // 2
    y_bits, z_bits = list(range(bits - 1, half, -1)), list(range(half, 0, -1))
    for pair in range(max(len(y_bits), len(z_bits))):
        if pair < len(y_bits):
            order.append(y_bits[pair])
        if pair < len(z_bits):
            order.append(z_bits[pair])
    order.append(0)
    held = block.T
    for bit in order:
        theirs = lax.ppermute(held, "ctx", [(i, i ^ (1 << bit)) for i in range(count)])
        upper = ((me >> bit) & 1) == 1
        lo = jnp.where(upper, theirs, held)
        hi = jnp.where(upper, held, theirs)
        held = jnp.stack([lo, hi], 0)
    axis_of = {bit: place for place, bit in enumerate(reversed(order))}
    perm = [axis_of[bit] for bit in range(bits - 1, -1, -1)] + [bits, bits + 1]
    return held.transpose(perm).reshape(count * block.shape[1], block.shape[0])


def attend(query_block, key_blk, value_blk, inside, sink_row_block, factor):
    score = (
        jnp.einsum("rgqd,sgd->gqrs", query_block, key_blk, preferred_element_type=jnp.float32)
        * factor
    )
    masked = jnp.where(inside, score, -1e30)
    top_score = jnp.maximum(jnp.max(masked, -1), sink_row_block[:, :, None])
    expvals = jnp.where(inside, jnp.exp(score - top_score[..., None]), 0.0)
    denominator = jnp.sum(expvals, -1) + jnp.exp(sink_row_block[:, :, None] - top_score)
    probs = (expvals / denominator[..., None]).astype(jnp.bfloat16)
    mixed = jnp.einsum("gqrs,sgd->rgqd", probs, value_blk, preferred_element_type=jnp.float32)
    return mixed.astype(jnp.bfloat16)


def body(
    hidden_in,
    queries,
    rotated_key_value,
    sink_logit_table,
    out_proj,
    norm_gain,
    expert_in,
    expert_out,
    routes,
    route_scores,
):
    tok_rows = hidden_in.shape[0]
    kv_heads = rotated_key_value.shape[1]
    head_dim = rotated_key_value.shape[2] // 2
    q_heads = sink_logit_table.shape[0]
    queries_per_group = q_heads // kv_heads
    factor = head_dim ** (-0.5)
    sink_row_block = sink_logit_table.reshape(kv_heads, queries_per_group)
    earlier = shifted(rotated_key_value, "ctx", 1)
    keys_all = jnp.concatenate([earlier, rotated_key_value], 0)
    first_pos = lax.axis_index("ctx") * tok_rows
    block_row_count = min(512, tok_rows)
    query_block = queries.reshape(block_row_count, kv_heads, queries_per_group, head_dim)
    query_pos = first_pos + 0 + jnp.arange(block_row_count, dtype=jnp.int32)[:, None]
    key_pos = (
        first_pos
        + 0
        - WINDOW_KEYS
        + jnp.arange(block_row_count + WINDOW_KEYS, dtype=jnp.int32)[None, :]
    )
    inside = (key_pos <= query_pos) & (key_pos > query_pos - WINDOW_KEYS) & (key_pos >= 0)
    mixed = attend(
        query_block,
        keys_all[..., :head_dim],
        keys_all[..., head_dim:],
        inside,
        sink_row_block,
        factor,
    )
    outputs = mixed.reshape(block_row_count, q_heads * head_dim)
    head_partial = lax.dot_general(
        outputs,
        gathered_columns(out_proj),
        (((1,), (1,)), ((), ())),
        preferred_element_type=jnp.float32,
    )
    d_model = head_partial.shape[1]
    residual = hidden_in.astype(jnp.float32) + lax.psum_scatter(
        head_partial.astype(jnp.bfloat16), "tp", scatter_dimension=1, tiled=True
    ).astype(jnp.float32)
    square_total = lax.psum(jnp.sum(residual * residual, -1), "tp")
    normed = (residual * lax.rsqrt(square_total[:, None] / d_model + 1e-05) * norm_gain).astype(
        jnp.bfloat16
    )
    ctx_count = lax.axis_size("ctx")
    tp_count = lax.axis_size("tp")
    top_count = routes.shape[1]
    experts = ctx_count * expert_in.shape[0]
    capacity = max(2, min(tok_rows, 3 * top_count * tok_rows // experts))
    quarter_w = d_model // tp_count
    onehot = (routes[:, :, None] == jnp.arange(experts, dtype=jnp.int32)).astype(jnp.int32)
    per_tok = jnp.sum(onehot, 1)
    before = jnp.cumsum(per_tok, axis=0) - per_tok
    slot_ids = jnp.sum(onehot * before[:, None, :], -1)
    flat_index = (routes * capacity + slot_ids).reshape(-1)
    weights = route_scores / jnp.sum(route_scores, -1, keepdims=True)
    tp_index = lax.axis_index("tp")
    spread = jnp.broadcast_to(normed[:, None, :], (tok_rows, top_count, quarter_w)).reshape(
        -1, quarter_w
    )
    outbox = jnp.zeros((experts * capacity, quarter_w), jnp.bfloat16).at[flat_index].set(spread)
    arrived = lax.all_to_all(
        outbox.reshape(ctx_count, capacity, quarter_w), "ctx", 0, 0, tiled=True
    ).reshape(-1, quarter_w)
    pieces = [arrived]
    for step in range(1, tp_count):
        pieces.append(lax.ppermute(arrived, "tp", [(i, (i + step) % tp_count) for i in range(tp_count)]))
    row_data = jnp.concatenate(pieces, 1)
    order = (tp_index - jnp.arange(tp_count, dtype=jnp.int32)) % tp_count
    hidden_w = expert_in.shape[3]
    w_gate = jnp.take(expert_in[0, 0].reshape(tp_count, quarter_w, hidden_w), order, axis=0).reshape(d_model, hidden_w)
    w_up = jnp.take(expert_in[0, 1].reshape(tp_count, quarter_w, hidden_w), order, axis=0).reshape(d_model, hidden_w)
    gate_vals = jnp.dot(row_data, w_gate, preferred_element_type=jnp.float32)
    up_vals = jnp.dot(row_data, w_up, preferred_element_type=jnp.float32)
    activated = ((up_vals + 1.0) * gate_vals * jax.nn.sigmoid(1.702 * gate_vals)).astype(
        jnp.bfloat16
    )
    def partial_for(quarter_id):
        cols = lax.dynamic_slice_in_dim(expert_out[0], quarter_id * quarter_w, quarter_w, 1)
        return jnp.dot(activated, cols, preferred_element_type=jnp.float32).astype(jnp.bfloat16)

    summed = partial_for(tp_index).astype(jnp.float32)
    for step in range(1, tp_count):
        piece = partial_for((tp_index + step) % tp_count)
        summed = summed + lax.ppermute(
            piece, "tp", [(i, (i + step) % tp_count) for i in range(tp_count)]
        ).astype(jnp.float32)
    result = summed.astype(jnp.bfloat16).reshape(ctx_count, capacity, quarter_w)
    returned = lax.all_to_all(result, "ctx", 0, 0, tiled=True).reshape(-1, quarter_w)
    expert_result = returned[flat_index].reshape(tok_rows, top_count, quarter_w)
    moe_sum = jnp.zeros((tok_rows, quarter_w), jnp.float32)
    for member in range(top_count):
        moe_sum = moe_sum + weights[:, member : member + 1] * expert_result[:, member].astype(
            jnp.float32
        )
    return (residual + moe_sum).astype(jnp.bfloat16)


def solution(mesh):
    in_specs = (
        P("ctx", "tp"),
        P("ctx", "tp"),
        P("ctx", "tp", None),
        P("tp"),
        P("tp", "ctx"),
        P("tp"),
        P("ctx", None, None, "tp"),
        P("ctx", "tp", None),
        P("ctx", None),
        P("ctx", None),
    )
    out_specs = P("ctx", "tp")
    return jax.shard_map(body, mesh=mesh, in_specs=in_specs, out_specs=out_specs, check_vma=False)
```

```python
import jax
import jax.numpy as jnp
from jax import lax
from jax.sharding import PartitionSpec as P

WINDOW_KEYS = 128


def shifted(value, axis, steps):
    count = lax.axis_size(axis)
    first, last = (max(0, -steps), min(count, count - steps))
    return lax.ppermute(value, axis, [(source, source + steps) for source in range(first, last)])


def gathered_columns(block):
    count = lax.axis_size("ctx")
    bits = count.bit_length() - 1
    me = lax.axis_index("ctx")
    order = []
    half = (bits - 1) // 2
    y_bits, z_bits = list(range(bits - 1, half, -1)), list(range(half, 0, -1))
    for pair in range(max(len(y_bits), len(z_bits))):
        if pair < len(y_bits):
            order.append(y_bits[pair])
        if pair < len(z_bits):
            order.append(z_bits[pair])
    order.append(0)
    held = block.T
    for bit in order:
        theirs = lax.ppermute(held, "ctx", [(i, i ^ (1 << bit)) for i in range(count)])
        upper = ((me >> bit) & 1) == 1
        lo = jnp.where(upper, theirs, held)
        hi = jnp.where(upper, held, theirs)
        held = jnp.stack([lo, hi], 0)
    axis_of = {bit: place for place, bit in enumerate(reversed(order))}
    perm = [axis_of[bit] for bit in range(bits - 1, -1, -1)] + [bits, bits + 1]
    return held.transpose(perm).reshape(count * block.shape[1], block.shape[0])


def attend(query_block, key_blk, value_blk, inside, sink_row_block, factor):
    score = (
        jnp.einsum("rgqd,sgd->gqrs", query_block, key_blk, preferred_element_type=jnp.float32)
        * factor
    )
    masked = jnp.where(inside, score, -1e30)
    top_score = jnp.maximum(jnp.max(masked, -1), sink_row_block[:, :, None])
    expvals = jnp.where(inside, jnp.exp(score - top_score[..., None]), 0.0)
    denominator = jnp.sum(expvals, -1) + jnp.exp(sink_row_block[:, :, None] - top_score)
    probs = (expvals / denominator[..., None]).astype(jnp.bfloat16)
    mixed = jnp.einsum("gqrs,sgd->rgqd", probs, value_blk, preferred_element_type=jnp.float32)
    return mixed.astype(jnp.bfloat16)


def body(
    hidden_in,
    queries,
    rotated_key_value,
    sink_logit_table,
    out_proj,
    norm_gain,
    expert_in,
    expert_out,
    routes,
    route_scores,
):
    tok_rows = hidden_in.shape[0]
    kv_heads = rotated_key_value.shape[1]
    head_dim = rotated_key_value.shape[2] // 2
    q_heads = sink_logit_table.shape[0]
    queries_per_group = q_heads // kv_heads
    factor = head_dim ** (-0.5)
    sink_row_block = sink_logit_table.reshape(kv_heads, queries_per_group)
    earlier = shifted(rotated_key_value, "ctx", 1)
    keys_all = jnp.concatenate([earlier, rotated_key_value], 0)
    first_pos = lax.axis_index("ctx") * tok_rows
    block_row_count = min(512, tok_rows)
    query_block = queries.reshape(block_row_count, kv_heads, queries_per_group, head_dim)
    query_pos = first_pos + 0 + jnp.arange(block_row_count, dtype=jnp.int32)[:, None]
    key_pos = (
        first_pos
        + 0
        - WINDOW_KEYS
        + jnp.arange(block_row_count + WINDOW_KEYS, dtype=jnp.int32)[None, :]
    )
    inside = (key_pos <= query_pos) & (key_pos > query_pos - WINDOW_KEYS) & (key_pos >= 0)
    mixed = attend(
        query_block,
        keys_all[..., :head_dim],
        keys_all[..., head_dim:],
        inside,
        sink_row_block,
        factor,
    )
    outputs = mixed.reshape(block_row_count, q_heads * head_dim)
    head_partial = lax.dot_general(
        outputs,
        gathered_columns(out_proj),
        (((1,), (1,)), ((), ())),
        preferred_element_type=jnp.float32,
    )
    d_model = head_partial.shape[1]
    tp_count = lax.axis_size("tp")
    tp_index = lax.axis_index("tp")
    quarter_w = d_model // tp_count
    sent = jnp.concatenate([head_partial.astype(jnp.bfloat16), hidden_in], 1)
    held = [(sent, tp_index)]
    for step in range(1, tp_count):
        got = lax.ppermute(sent, "tp", [(i, (i + step) % tp_count) for i in range(tp_count)])
        held.append((got, (tp_index - step) % tp_count))
    head_sum = held[0][0][:, :d_model].astype(jnp.float32)
    for got, _ in held[1:]:
        head_sum = head_sum + got[:, :d_model].astype(jnp.float32)
    square_total = jnp.zeros((tok_rows,), jnp.float32)
    residual = None
    for got, quarter_id in held:
        part = got[:, d_model:].astype(jnp.float32) + lax.dynamic_slice_in_dim(
            head_sum, quarter_id * quarter_w, quarter_w, 1
        )
        square_total = square_total + jnp.sum(part * part, -1)
        if residual is None:
            residual = part
    normed = (residual * lax.rsqrt(square_total[:, None] / d_model + 1e-05) * norm_gain).astype(
        jnp.bfloat16
    )
    ctx_count = lax.axis_size("ctx")
    top_count = routes.shape[1]
    experts = ctx_count * expert_in.shape[0]
    capacity = max(2, min(tok_rows, 3 * top_count * tok_rows // experts))
    onehot = (routes[:, :, None] == jnp.arange(experts, dtype=jnp.int32)).astype(jnp.int32)
    per_tok = jnp.sum(onehot, 1)
    before = jnp.cumsum(per_tok, axis=0) - per_tok
    slot_ids = jnp.sum(onehot * before[:, None, :], -1)
    flat_index = (routes * capacity + slot_ids).reshape(-1)
    weights = route_scores / jnp.sum(route_scores, -1, keepdims=True)
    spread = jnp.broadcast_to(normed[:, None, :], (tok_rows, top_count, quarter_w)).reshape(
        -1, quarter_w
    )
    outbox = jnp.zeros((experts * capacity, quarter_w), jnp.bfloat16).at[flat_index].set(spread)
    arrived = lax.all_to_all(
        outbox.reshape(ctx_count, capacity, quarter_w), "ctx", 0, 0, tiled=True
    ).reshape(-1, quarter_w)
    pieces = [(arrived, tp_index)]
    for step in range(1, tp_count):
        got = lax.ppermute(arrived, "tp", [(i, (i + step) % tp_count) for i in range(tp_count)])
        pieces.append((got, (tp_index - step) % tp_count))
    gate_vals = None
    up_vals = None
    for piece, quarter_id in pieces:
        rows_of = lambda w: lax.dynamic_slice_in_dim(w, quarter_id * quarter_w, quarter_w, 0)
        gate_part = jnp.dot(piece, rows_of(expert_in[0, 0]), preferred_element_type=jnp.float32)
        up_part = jnp.dot(piece, rows_of(expert_in[0, 1]), preferred_element_type=jnp.float32)
        gate_vals = gate_part if gate_vals is None else gate_vals + gate_part
        up_vals = up_part if up_vals is None else up_vals + up_part
    activated = ((up_vals + 1.0) * gate_vals * jax.nn.sigmoid(1.702 * gate_vals)).astype(
        jnp.bfloat16
    )
    def partial_for(quarter_id):
        cols = lax.dynamic_slice_in_dim(expert_out[0], quarter_id * quarter_w, quarter_w, 1)
        return jnp.dot(activated, cols, preferred_element_type=jnp.float32).astype(jnp.bfloat16)

    arriving = []
    for step in range(1, tp_count):
        piece = partial_for((tp_index + step) % tp_count)
        arriving.append(
            lax.ppermute(piece, "tp", [(i, (i + step) % tp_count) for i in range(tp_count)])
        )
    summed = partial_for(tp_index).astype(jnp.float32)
    for got in arriving:
        summed = summed + got.astype(jnp.float32)
    result = summed.astype(jnp.bfloat16).reshape(ctx_count, capacity, quarter_w)
    returned = lax.all_to_all(result, "ctx", 0, 0, tiled=True).reshape(-1, quarter_w)
    expert_result = returned[flat_index].reshape(tok_rows, top_count, quarter_w)
    moe_sum = jnp.zeros((tok_rows, quarter_w), jnp.float32)
    for member in range(top_count):
        moe_sum = moe_sum + weights[:, member : member + 1] * expert_result[:, member].astype(
            jnp.float32
        )
    return (residual + moe_sum).astype(jnp.bfloat16)


def solution(mesh):
    in_specs = (
        P("ctx", "tp"),
        P("ctx", "tp"),
        P("ctx", "tp", None),
        P("tp"),
        P("tp", "ctx"),
        P("tp"),
        P("ctx", None, None, "tp"),
        P("ctx", "tp", None),
        P("ctx", None),
        P("ctx", None),
    )
    out_specs = P("ctx", "tp")
    return jax.shard_map(body, mesh=mesh, in_specs=in_specs, out_specs=out_specs, check_vma=False)
```

```python
import jax
import jax.numpy as jnp
from jax import lax
from jax.sharding import PartitionSpec as P

WINDOW_KEYS = 128


def shifted(value, axis, steps):
    count = lax.axis_size(axis)
    first, last = (max(0, -steps), min(count, count - steps))
    return lax.ppermute(value, axis, [(source, source + steps) for source in range(first, last)])


def gathered_columns(block):
    count = lax.axis_size("ctx")
    bits = count.bit_length() - 1
    me = lax.axis_index("ctx")
    order = []
    half = (bits - 1) // 2
    y_bits, z_bits = list(range(bits - 1, half, -1)), list(range(half, 0, -1))
    for pair in range(max(len(y_bits), len(z_bits))):
        if pair < len(y_bits):
            order.append(y_bits[pair])
        if pair < len(z_bits):
            order.append(z_bits[pair])
    order.append(0)
    held = block.T
    for bit in order:
        theirs = lax.ppermute(held, "ctx", [(i, i ^ (1 << bit)) for i in range(count)])
        upper = ((me >> bit) & 1) == 1
        lo = jnp.where(upper, theirs, held)
        hi = jnp.where(upper, held, theirs)
        held = jnp.stack([lo, hi], 0)
    axis_of = {bit: place for place, bit in enumerate(reversed(order))}
    perm = [axis_of[bit] for bit in range(bits - 1, -1, -1)] + [bits, bits + 1]
    return held.transpose(perm).reshape(count * block.shape[1], block.shape[0])


def attend(query_block, key_blk, value_blk, inside, sink_row_block, factor):
    score = (
        jnp.einsum("rgqd,sgd->gqrs", query_block, key_blk, preferred_element_type=jnp.float32)
        * factor
    )
    masked = jnp.where(inside, score, -1e30)
    top_score = jnp.maximum(jnp.max(masked, -1), sink_row_block[:, :, None])
    expvals = jnp.where(inside, jnp.exp(score - top_score[..., None]), 0.0)
    denominator = jnp.sum(expvals, -1) + jnp.exp(sink_row_block[:, :, None] - top_score)
    probs = (expvals / denominator[..., None]).astype(jnp.bfloat16)
    mixed = jnp.einsum("gqrs,sgd->rgqd", probs, value_blk, preferred_element_type=jnp.float32)
    return mixed.astype(jnp.bfloat16)


def body(
    hidden_in,
    queries,
    rotated_key_value,
    sink_logit_table,
    out_proj,
    norm_gain,
    expert_in,
    expert_out,
    routes,
    route_scores,
):
    tok_rows = hidden_in.shape[0]
    kv_heads = rotated_key_value.shape[1]
    head_dim = rotated_key_value.shape[2] // 2
    q_heads = sink_logit_table.shape[0]
    queries_per_group = q_heads // kv_heads
    factor = head_dim ** (-0.5)
    sink_row_block = sink_logit_table.reshape(kv_heads, queries_per_group)
    earlier = shifted(rotated_key_value, "ctx", 1)
    keys_all = jnp.concatenate([earlier, rotated_key_value], 0)
    first_pos = lax.axis_index("ctx") * tok_rows
    block_row_count = min(512, tok_rows)
    query_block = queries.reshape(block_row_count, kv_heads, queries_per_group, head_dim)
    query_pos = first_pos + 0 + jnp.arange(block_row_count, dtype=jnp.int32)[:, None]
    key_pos = (
        first_pos
        + 0
        - WINDOW_KEYS
        + jnp.arange(block_row_count + WINDOW_KEYS, dtype=jnp.int32)[None, :]
    )
    inside = (key_pos <= query_pos) & (key_pos > query_pos - WINDOW_KEYS) & (key_pos >= 0)
    mixed = attend(
        query_block,
        keys_all[..., :head_dim],
        keys_all[..., head_dim:],
        inside,
        sink_row_block,
        factor,
    )
    outputs = mixed.reshape(block_row_count, q_heads * head_dim)
    head_partial = lax.dot_general(
        outputs,
        gathered_columns(out_proj),
        (((1,), (1,)), ((), ())),
        preferred_element_type=jnp.float32,
    )
    d_model = head_partial.shape[1]
    tp_count = lax.axis_size("tp")
    tp_index = lax.axis_index("tp")
    quarter_w = d_model // tp_count
    sent = jnp.concatenate([head_partial.astype(jnp.bfloat16), hidden_in], 1)
    held = [(sent, tp_index)]
    for step in range(1, tp_count):
        got = lax.ppermute(sent, "tp", [(i, (i + step) % tp_count) for i in range(tp_count)])
        held.append((got, (tp_index - step) % tp_count))
    head_sum = held[0][0][:, :d_model].astype(jnp.float32)
    for got, _ in held[1:]:
        head_sum = head_sum + got[:, :d_model].astype(jnp.float32)
    square_total = jnp.zeros((tok_rows,), jnp.float32)
    residual = None
    for got, quarter_id in held:
        part = got[:, d_model:].astype(jnp.float32) + lax.dynamic_slice_in_dim(
            head_sum, quarter_id * quarter_w, quarter_w, 1
        )
        square_total = square_total + jnp.sum(part * part, -1)
        if residual is None:
            residual = part
    normed = (residual * lax.rsqrt(square_total[:, None] / d_model + 1e-05) * norm_gain).astype(
        jnp.bfloat16
    )
    ctx_count = lax.axis_size("ctx")
    top_count = routes.shape[1]
    experts = ctx_count * expert_in.shape[0]
    capacity = max(2, min(tok_rows, 3 * top_count * tok_rows // experts))
    onehot = (routes[:, :, None] == jnp.arange(experts, dtype=jnp.int32)).astype(jnp.int32)
    per_tok = jnp.sum(onehot, 1)
    before = jnp.cumsum(per_tok, axis=0) - per_tok
    slot_ids = jnp.sum(onehot * before[:, None, :], -1)
    flat_index = (routes * capacity + slot_ids).reshape(-1)
    weights = route_scores / jnp.sum(route_scores, -1, keepdims=True)
    spread = jnp.broadcast_to(normed[:, None, :], (tok_rows, top_count, quarter_w)).reshape(
        -1, quarter_w
    )
    outbox = jnp.zeros((experts * capacity, quarter_w), jnp.bfloat16).at[flat_index].set(spread)
    arrived = lax.all_to_all(
        outbox.reshape(ctx_count, capacity, quarter_w), "ctx", 0, 0, tiled=True
    ).reshape(-1, quarter_w)
    assert tp_count == 4
    ahead = [(i, (i + 1) % tp_count) for i in range(tp_count)]
    behind = [(i, (i - 1) % tp_count) for i in range(tp_count)]
    half_rows = arrived.shape[0] // 2
    from_behind = lax.ppermute(arrived, "tp", ahead)
    from_ahead = lax.ppermute(arrived, "tp", behind)
    first_half = lax.ppermute(from_behind[:half_rows], "tp", ahead)
    second_half = lax.ppermute(from_ahead[half_rows:], "tp", behind)
    opposite = jnp.concatenate([first_half, second_half], 0)
    pieces = [
        (arrived, tp_index),
        (from_behind, (tp_index - 1) % tp_count),
        (from_ahead, (tp_index + 1) % tp_count),
        (opposite, (tp_index + 2) % tp_count),
    ]
    gate_vals = None
    up_vals = None
    for piece, quarter_id in pieces:
        rows_of = lambda w: lax.dynamic_slice_in_dim(w, quarter_id * quarter_w, quarter_w, 0)
        gate_part = jnp.dot(piece, rows_of(expert_in[0, 0]), preferred_element_type=jnp.float32)
        up_part = jnp.dot(piece, rows_of(expert_in[0, 1]), preferred_element_type=jnp.float32)
        gate_vals = gate_part if gate_vals is None else gate_vals + gate_part
        up_vals = up_part if up_vals is None else up_vals + up_part
    activated = ((up_vals + 1.0) * gate_vals * jax.nn.sigmoid(1.702 * gate_vals)).astype(
        jnp.bfloat16
    )
    def partial_for(quarter_id):
        cols = lax.dynamic_slice_in_dim(expert_out[0], quarter_id * quarter_w, quarter_w, 1)
        return jnp.dot(activated, cols, preferred_element_type=jnp.float32).astype(jnp.bfloat16)

    across = partial_for((tp_index + 2) % tp_count)
    via_ahead = lax.ppermute(across[:half_rows], "tp", ahead)
    via_behind = lax.ppermute(across[half_rows:], "tp", behind)
    for_ahead = partial_for((tp_index + 1) % tp_count).astype(jnp.float32)
    for_ahead = jnp.concatenate(
        [for_ahead[:half_rows] + via_ahead.astype(jnp.float32), for_ahead[half_rows:]], 0
    ).astype(jnp.bfloat16)
    for_behind = partial_for((tp_index - 1) % tp_count).astype(jnp.float32)
    for_behind = jnp.concatenate(
        [for_behind[:half_rows], for_behind[half_rows:] + via_behind.astype(jnp.float32)], 0
    ).astype(jnp.bfloat16)
    got_behind = lax.ppermute(for_ahead, "tp", ahead)
    got_ahead = lax.ppermute(for_behind, "tp", behind)
    summed = (
        partial_for(tp_index).astype(jnp.float32)
        + got_behind.astype(jnp.float32)
        + got_ahead.astype(jnp.float32)
    )
    result = summed.astype(jnp.bfloat16).reshape(ctx_count, capacity, quarter_w)
    returned = lax.all_to_all(result, "ctx", 0, 0, tiled=True).reshape(-1, quarter_w)
    expert_result = returned[flat_index].reshape(tok_rows, top_count, quarter_w)
    moe_sum = jnp.zeros((tok_rows, quarter_w), jnp.float32)
    for member in range(top_count):
        moe_sum = moe_sum + weights[:, member : member + 1] * expert_result[:, member].astype(
            jnp.float32
        )
    return (residual + moe_sum).astype(jnp.bfloat16)


def solution(mesh):
    in_specs = (
        P("ctx", "tp"),
        P("ctx", "tp"),
        P("ctx", "tp", None),
        P("tp"),
        P("tp", "ctx"),
        P("tp"),
        P("ctx", None, None, "tp"),
        P("ctx", "tp", None),
        P("ctx", None),
        P("ctx", None),
    )
    out_specs = P("ctx", "tp")
    return jax.shard_map(body, mesh=mesh, in_specs=in_specs, out_specs=out_specs, check_vma=False)
```

```python
import jax
import jax.numpy as jnp
from jax import lax
from jax.sharding import Mesh, PartitionSpec as P

WINDOW_KEYS = 128


CTX = ("yz", "core")


def ctx_size():
    return lax.axis_size("yz") * lax.axis_size("core")


def shifted(value, steps):
    count = ctx_size()
    first, last = (max(0, -steps), min(count, count - steps))
    return lax.ppermute(value, CTX, [(source, source + steps) for source in range(first, last)])


def by_core(mine, theirs):
    first = lax.axis_index("core") == 0
    return jnp.stack([jnp.where(first, mine, theirs), jnp.where(first, theirs, mine)], 1)


def other_core(value):
    return lax.ppermute(value, "core", [(0, 1), (1, 0)])


def gathered_columns(block):
    rows = block.T
    spread = jnp.broadcast_to(rows[None], (lax.axis_size("yz"),) + rows.shape)
    mine = lax.all_to_all(spread, "yz", 0, 0, tiled=True)
    return by_core(mine, other_core(mine)).reshape(-1, rows.shape[1])


def to_experts(outbox):
    parts = outbox.reshape((lax.axis_size("yz"), 2) + outbox.shape[1:])
    first = lax.axis_index("core") == 0
    mine = jnp.where(first, parts[:, 0], parts[:, 1])
    theirs = jnp.where(first, parts[:, 1], parts[:, 0])
    staged = by_core(mine, other_core(theirs))
    return lax.all_to_all(staged, "yz", 0, 0, tiled=True).reshape(outbox.shape)


def from_experts(result):
    parts = result.reshape((lax.axis_size("yz"), 2) + result.shape[1:])
    staged = lax.all_to_all(parts, "yz", 0, 0, tiled=True)
    first = lax.axis_index("core") == 0
    mine = jnp.where(first, staged[:, 0], staged[:, 1])
    theirs = jnp.where(first, staged[:, 1], staged[:, 0])
    return by_core(mine, other_core(theirs)).reshape(result.shape)


def attend(query_block, key_blk, value_blk, inside, sink_row_block, factor):
    score = (
        jnp.einsum("rgqd,sgd->gqrs", query_block, key_blk, preferred_element_type=jnp.float32)
        * factor
    )
    masked = jnp.where(inside, score, -1e30)
    top_score = jnp.maximum(jnp.max(masked, -1), sink_row_block[:, :, None])
    expvals = jnp.where(inside, jnp.exp(score - top_score[..., None]), 0.0)
    denominator = jnp.sum(expvals, -1) + jnp.exp(sink_row_block[:, :, None] - top_score)
    probs = (expvals / denominator[..., None]).astype(jnp.bfloat16)
    mixed = jnp.einsum("gqrs,sgd->rgqd", probs, value_blk, preferred_element_type=jnp.float32)
    return mixed.astype(jnp.bfloat16)


def body(
    hidden_in,
    queries,
    rotated_key_value,
    sink_logit_table,
    out_proj,
    norm_gain,
    expert_in,
    expert_out,
    routes,
    route_scores,
):
    tok_rows = hidden_in.shape[0]
    kv_heads = rotated_key_value.shape[1]
    head_dim = rotated_key_value.shape[2] // 2
    q_heads = sink_logit_table.shape[0]
    queries_per_group = q_heads // kv_heads
    factor = head_dim ** (-0.5)
    sink_row_block = sink_logit_table.reshape(kv_heads, queries_per_group)
    earlier = shifted(rotated_key_value, 1)
    keys_all = jnp.concatenate([earlier, rotated_key_value], 0)
    first_pos = lax.axis_index(CTX) * tok_rows
    block_row_count = min(512, tok_rows)
    query_block = queries.reshape(block_row_count, kv_heads, queries_per_group, head_dim)
    query_pos = first_pos + 0 + jnp.arange(block_row_count, dtype=jnp.int32)[:, None]
    key_pos = (
        first_pos
        + 0
        - WINDOW_KEYS
        + jnp.arange(block_row_count + WINDOW_KEYS, dtype=jnp.int32)[None, :]
    )
    inside = (key_pos <= query_pos) & (key_pos > query_pos - WINDOW_KEYS) & (key_pos >= 0)
    mixed = attend(
        query_block,
        keys_all[..., :head_dim],
        keys_all[..., head_dim:],
        inside,
        sink_row_block,
        factor,
    )
    outputs = mixed.reshape(block_row_count, q_heads * head_dim)
    head_partial = lax.dot_general(
        outputs,
        gathered_columns(out_proj),
        (((1,), (1,)), ((), ())),
        preferred_element_type=jnp.float32,
    )
    d_model = head_partial.shape[1]
    tp_count = lax.axis_size("tp")
    tp_index = lax.axis_index("tp")
    quarter_w = d_model // tp_count
    sent = jnp.concatenate([head_partial.astype(jnp.bfloat16), hidden_in], 1)
    assert tp_count == 4
    ahead = [(i, (i + 1) % tp_count) for i in range(tp_count)]
    behind = [(i, (i - 1) % tp_count) for i in range(tp_count)]
    from_behind = lax.ppermute(sent, "tp", ahead)
    from_ahead = lax.ppermute(sent, "tp", behind)
    half_tok = tok_rows // 2
    opposite = jnp.concatenate(
        [
            lax.ppermute(from_behind[:half_tok], "tp", ahead),
            lax.ppermute(from_ahead[half_tok:], "tp", behind),
        ],
        0,
    )
    held = [
        (sent, tp_index),
        (from_behind, (tp_index - 1) % tp_count),
        (from_ahead, (tp_index + 1) % tp_count),
        (opposite, (tp_index + 2) % tp_count),
    ]
    head_sum = held[0][0][:, :d_model].astype(jnp.float32)
    for got, _ in held[1:]:
        head_sum = head_sum + got[:, :d_model].astype(jnp.float32)
    square_total = jnp.zeros((tok_rows,), jnp.float32)
    residual = None
    for got, quarter_id in held:
        part = got[:, d_model:].astype(jnp.float32) + lax.dynamic_slice_in_dim(
            head_sum, quarter_id * quarter_w, quarter_w, 1
        )
        square_total = square_total + jnp.sum(part * part, -1)
        if residual is None:
            residual = part
    normed = (residual * lax.rsqrt(square_total[:, None] / d_model + 1e-05) * norm_gain).astype(
        jnp.bfloat16
    )
    ctx_count = ctx_size()
    top_count = routes.shape[1]
    experts = ctx_count * expert_in.shape[0]
    capacity = max(2, min(tok_rows, 3 * top_count * tok_rows // experts))
    onehot = (routes[:, :, None] == jnp.arange(experts, dtype=jnp.int32)).astype(jnp.int32)
    per_tok = jnp.sum(onehot, 1)
    before = jnp.cumsum(per_tok, axis=0) - per_tok
    slot_ids = jnp.sum(onehot * before[:, None, :], -1)
    flat_index = (routes * capacity + slot_ids).reshape(-1)
    weights = route_scores / jnp.sum(route_scores, -1, keepdims=True)
    spread = jnp.broadcast_to(normed[:, None, :], (tok_rows, top_count, quarter_w)).reshape(
        -1, quarter_w
    )
    outbox = jnp.zeros((experts * capacity, quarter_w), jnp.bfloat16).at[flat_index].set(spread)
    arrived = lax.all_to_all(outbox.reshape(ctx_count, capacity, quarter_w), CTX, 0, 0, tiled=True).reshape(-1, quarter_w)
    half_rows = arrived.shape[0] // 2
    from_behind = lax.ppermute(arrived, "tp", ahead)
    from_ahead = lax.ppermute(arrived, "tp", behind)
    first_half = lax.ppermute(from_behind[:half_rows], "tp", ahead)
    second_half = lax.ppermute(from_ahead[half_rows:], "tp", behind)
    opposite = jnp.concatenate([first_half, second_half], 0)
    pieces = [
        (arrived, tp_index),
        (from_behind, (tp_index - 1) % tp_count),
        (from_ahead, (tp_index + 1) % tp_count),
        (opposite, (tp_index + 2) % tp_count),
    ]
    gate_vals = None
    up_vals = None
    for piece, quarter_id in pieces:
        rows_of = lambda w: lax.dynamic_slice_in_dim(w, quarter_id * quarter_w, quarter_w, 0)
        gate_part = jnp.dot(piece, rows_of(expert_in[0, 0]), preferred_element_type=jnp.float32)
        up_part = jnp.dot(piece, rows_of(expert_in[0, 1]), preferred_element_type=jnp.float32)
        gate_vals = gate_part if gate_vals is None else gate_vals + gate_part
        up_vals = up_part if up_vals is None else up_vals + up_part
    activated = ((up_vals + 1.0) * gate_vals * jax.nn.sigmoid(1.702 * gate_vals)).astype(
        jnp.bfloat16
    )
    def partial_for(quarter_id):
        cols = lax.dynamic_slice_in_dim(expert_out[0], quarter_id * quarter_w, quarter_w, 1)
        return jnp.dot(activated, cols, preferred_element_type=jnp.float32).astype(jnp.bfloat16)

    across = partial_for((tp_index + 2) % tp_count)
    via_ahead = lax.ppermute(across[:half_rows], "tp", ahead)
    via_behind = lax.ppermute(across[half_rows:], "tp", behind)
    for_ahead = partial_for((tp_index + 1) % tp_count).astype(jnp.float32)
    for_ahead = jnp.concatenate(
        [for_ahead[:half_rows] + via_ahead.astype(jnp.float32), for_ahead[half_rows:]], 0
    ).astype(jnp.bfloat16)
    for_behind = partial_for((tp_index - 1) % tp_count).astype(jnp.float32)
    for_behind = jnp.concatenate(
        [for_behind[:half_rows], for_behind[half_rows:] + via_behind.astype(jnp.float32)], 0
    ).astype(jnp.bfloat16)
    got_behind = lax.ppermute(for_ahead, "tp", ahead)
    got_ahead = lax.ppermute(for_behind, "tp", behind)
    summed = (
        partial_for(tp_index).astype(jnp.float32)
        + got_behind.astype(jnp.float32)
        + got_ahead.astype(jnp.float32)
    )
    result = summed.astype(jnp.bfloat16).reshape(ctx_count, capacity, quarter_w)
    returned = lax.all_to_all(result, CTX, 0, 0, tiled=True).reshape(-1, quarter_w)
    expert_result = returned[flat_index].reshape(tok_rows, top_count, quarter_w)
    moe_sum = jnp.zeros((tok_rows, quarter_w), jnp.float32)
    for member in range(top_count):
        moe_sum = moe_sum + weights[:, member : member + 1] * expert_result[:, member].astype(
            jnp.float32
        )
    return (residual + moe_sum).astype(jnp.bfloat16)


def solution(mesh):
    chips = mesh.devices.reshape(mesh.shape["ctx"] // 2, 2, mesh.shape["tp"])
    split = Mesh(chips, ("yz", "core", "tp"))
    in_specs = (
        P(CTX, "tp"),
        P(CTX, "tp"),
        P(CTX, "tp", None),
        P("tp"),
        P("tp", CTX),
        P("tp"),
        P(CTX, None, None, "tp"),
        P(CTX, "tp", None),
        P(CTX, None),
        P(CTX, None),
    )
    out_specs = P(CTX, "tp")
    return jax.shard_map(body, mesh=split, in_specs=in_specs, out_specs=out_specs, check_vma=False)
```

```python
import jax
import jax.numpy as jnp
from jax import lax
from jax.sharding import Mesh, PartitionSpec as P

WINDOW_KEYS = 128


CTX = ("yz", "core")


def ctx_size():
    return lax.axis_size("yz") * lax.axis_size("core")


def shifted(value, steps):
    count = ctx_size()
    first, last = (max(0, -steps), min(count, count - steps))
    return lax.ppermute(value, CTX, [(source, source + steps) for source in range(first, last)])


def by_core(mine, theirs):
    first = lax.axis_index("core") == 0
    return jnp.stack([jnp.where(first, mine, theirs), jnp.where(first, theirs, mine)], 1)


def other_core(value):
    return lax.ppermute(value, "core", [(0, 1), (1, 0)])


def gathered_columns(block):
    rows = block.T
    spread = jnp.broadcast_to(rows[None], (lax.axis_size("yz"),) + rows.shape)
    mine = lax.all_to_all(spread, "yz", 0, 0, tiled=True)
    return by_core(mine, other_core(mine)).reshape(-1, rows.shape[1])


def to_experts(outbox):
    parts = outbox.reshape((lax.axis_size("yz"), 2) + outbox.shape[1:])
    first = lax.axis_index("core") == 0
    mine = jnp.where(first, parts[:, 0], parts[:, 1])
    theirs = jnp.where(first, parts[:, 1], parts[:, 0])
    staged = by_core(mine, other_core(theirs))
    return lax.all_to_all(staged, "yz", 0, 0, tiled=True).reshape(outbox.shape)


def from_experts(result):
    parts = result.reshape((lax.axis_size("yz"), 2) + result.shape[1:])
    staged = lax.all_to_all(parts, "yz", 0, 0, tiled=True)
    first = lax.axis_index("core") == 0
    mine = jnp.where(first, staged[:, 0], staged[:, 1])
    theirs = jnp.where(first, staged[:, 1], staged[:, 0])
    return by_core(mine, other_core(theirs)).reshape(result.shape)


def attend(query_block, key_blk, value_blk, inside, sink_row_block, factor):
    score = (
        jnp.einsum("rgqd,sgd->gqrs", query_block, key_blk, preferred_element_type=jnp.float32)
        * factor
    )
    masked = jnp.where(inside, score, -1e30)
    top_score = jnp.maximum(jnp.max(masked, -1), sink_row_block[:, :, None])
    expvals = jnp.where(inside, jnp.exp(score - top_score[..., None]), 0.0)
    denominator = jnp.sum(expvals, -1) + jnp.exp(sink_row_block[:, :, None] - top_score)
    probs = (expvals / denominator[..., None]).astype(jnp.bfloat16)
    mixed = jnp.einsum("gqrs,sgd->rgqd", probs, value_blk, preferred_element_type=jnp.float32)
    return mixed.astype(jnp.bfloat16)


def body(
    hidden_in,
    queries,
    rotated_key_value,
    sink_logit_table,
    out_proj,
    norm_gain,
    expert_in,
    expert_out,
    routes,
    route_scores,
):
    tok_rows = hidden_in.shape[0]
    kv_heads = rotated_key_value.shape[1]
    head_dim = rotated_key_value.shape[2] // 2
    q_heads = sink_logit_table.shape[0]
    queries_per_group = q_heads // kv_heads
    factor = head_dim ** (-0.5)
    sink_row_block = sink_logit_table.reshape(kv_heads, queries_per_group)
    earlier = shifted(rotated_key_value, 1)
    keys_all = jnp.concatenate([earlier, rotated_key_value], 0)
    first_pos = lax.axis_index(CTX) * tok_rows
    block_row_count = min(512, tok_rows)
    query_block = queries.reshape(block_row_count, kv_heads, queries_per_group, head_dim)
    query_pos = first_pos + 0 + jnp.arange(block_row_count, dtype=jnp.int32)[:, None]
    key_pos = (
        first_pos
        + 0
        - WINDOW_KEYS
        + jnp.arange(block_row_count + WINDOW_KEYS, dtype=jnp.int32)[None, :]
    )
    inside = (key_pos <= query_pos) & (key_pos > query_pos - WINDOW_KEYS) & (key_pos >= 0)
    mixed = attend(
        query_block,
        keys_all[..., :head_dim],
        keys_all[..., head_dim:],
        inside,
        sink_row_block,
        factor,
    )
    outputs = mixed.reshape(block_row_count, q_heads * head_dim)
    head_partial = lax.dot_general(
        outputs,
        gathered_columns(out_proj),
        (((1,), (1,)), ((), ())),
        preferred_element_type=jnp.float32,
    )
    d_model = head_partial.shape[1]
    tp_count = lax.axis_size("tp")
    tp_index = lax.axis_index("tp")
    quarter_w = d_model // tp_count
    sent = jnp.concatenate([head_partial.astype(jnp.bfloat16), hidden_in], 1)
    assert tp_count == 4
    ahead = [(i, (i + 1) % tp_count) for i in range(tp_count)]
    behind = [(i, (i - 1) % tp_count) for i in range(tp_count)]
    from_behind = lax.ppermute(sent, "tp", ahead)
    from_ahead = lax.ppermute(sent, "tp", behind)
    half_tok = tok_rows // 2
    opposite = jnp.concatenate(
        [
            lax.ppermute(from_behind[:half_tok], "tp", ahead),
            lax.ppermute(from_ahead[half_tok:], "tp", behind),
        ],
        0,
    )
    held = [
        (sent, tp_index),
        (from_behind, (tp_index - 1) % tp_count),
        (from_ahead, (tp_index + 1) % tp_count),
        (opposite, (tp_index + 2) % tp_count),
    ]
    head_sum = held[0][0][:, :d_model].astype(jnp.float32)
    for got, _ in held[1:]:
        head_sum = head_sum + got[:, :d_model].astype(jnp.float32)
    square_total = jnp.zeros((tok_rows,), jnp.float32)
    residual = None
    for got, quarter_id in held:
        part = got[:, d_model:].astype(jnp.float32) + lax.dynamic_slice_in_dim(
            head_sum, quarter_id * quarter_w, quarter_w, 1
        )
        square_total = square_total + jnp.sum(part * part, -1)
        if residual is None:
            residual = part
    normed = (residual * lax.rsqrt(square_total[:, None] / d_model + 1e-05) * norm_gain).astype(
        jnp.bfloat16
    )
    ctx_count = ctx_size()
    top_count = routes.shape[1]
    experts = ctx_count * expert_in.shape[0]
    capacity = max(2, min(tok_rows, 3 * top_count * tok_rows // experts))
    onehot = (routes[:, :, None] == jnp.arange(experts, dtype=jnp.int32)).astype(jnp.int32)
    per_tok = jnp.sum(onehot, 1)
    before = jnp.cumsum(per_tok, axis=0) - per_tok
    slot_ids = jnp.sum(onehot * before[:, None, :], -1)
    flat_index = (routes * capacity + slot_ids).reshape(-1)
    weights = route_scores / jnp.sum(route_scores, -1, keepdims=True)
    spread = jnp.broadcast_to(normed[:, None, :], (tok_rows, top_count, quarter_w)).reshape(
        -1, quarter_w
    )
    outbox = jnp.zeros((experts * capacity, quarter_w), jnp.bfloat16).at[flat_index].set(spread)
    arrived = to_experts(outbox.reshape(ctx_count, capacity, quarter_w)).reshape(-1, quarter_w)
    half_rows = arrived.shape[0] // 2
    from_behind = lax.ppermute(arrived, "tp", ahead)
    from_ahead = lax.ppermute(arrived, "tp", behind)
    first_half = lax.ppermute(from_behind[:half_rows], "tp", ahead)
    second_half = lax.ppermute(from_ahead[half_rows:], "tp", behind)
    opposite = jnp.concatenate([first_half, second_half], 0)
    pieces = [
        (arrived, tp_index),
        (from_behind, (tp_index - 1) % tp_count),
        (from_ahead, (tp_index + 1) % tp_count),
        (opposite, (tp_index + 2) % tp_count),
    ]
    gate_vals = None
    up_vals = None
    for piece, quarter_id in pieces:
        rows_of = lambda w: lax.dynamic_slice_in_dim(w, quarter_id * quarter_w, quarter_w, 0)
        gate_part = jnp.dot(piece, rows_of(expert_in[0, 0]), preferred_element_type=jnp.float32)
        up_part = jnp.dot(piece, rows_of(expert_in[0, 1]), preferred_element_type=jnp.float32)
        gate_vals = gate_part if gate_vals is None else gate_vals + gate_part
        up_vals = up_part if up_vals is None else up_vals + up_part
    activated = ((up_vals + 1.0) * gate_vals * jax.nn.sigmoid(1.702 * gate_vals)).astype(
        jnp.bfloat16
    )
    def partial_for(quarter_id):
        cols = lax.dynamic_slice_in_dim(expert_out[0], quarter_id * quarter_w, quarter_w, 1)
        return jnp.dot(activated, cols, preferred_element_type=jnp.float32).astype(jnp.bfloat16)

    across = partial_for((tp_index + 2) % tp_count)
    via_ahead = lax.ppermute(across[:half_rows], "tp", ahead)
    via_behind = lax.ppermute(across[half_rows:], "tp", behind)
    for_ahead = partial_for((tp_index + 1) % tp_count).astype(jnp.float32)
    for_ahead = jnp.concatenate(
        [for_ahead[:half_rows] + via_ahead.astype(jnp.float32), for_ahead[half_rows:]], 0
    ).astype(jnp.bfloat16)
    for_behind = partial_for((tp_index - 1) % tp_count).astype(jnp.float32)
    for_behind = jnp.concatenate(
        [for_behind[:half_rows], for_behind[half_rows:] + via_behind.astype(jnp.float32)], 0
    ).astype(jnp.bfloat16)
    got_behind = lax.ppermute(for_ahead, "tp", ahead)
    got_ahead = lax.ppermute(for_behind, "tp", behind)
    summed = (
        partial_for(tp_index).astype(jnp.float32)
        + got_behind.astype(jnp.float32)
        + got_ahead.astype(jnp.float32)
    )
    result = summed.astype(jnp.bfloat16).reshape(ctx_count, capacity, quarter_w)
    returned = lax.all_to_all(result, CTX, 0, 0, tiled=True).reshape(-1, quarter_w)
    expert_result = returned[flat_index].reshape(tok_rows, top_count, quarter_w)
    moe_sum = jnp.zeros((tok_rows, quarter_w), jnp.float32)
    for member in range(top_count):
        moe_sum = moe_sum + weights[:, member : member + 1] * expert_result[:, member].astype(
            jnp.float32
        )
    return (residual + moe_sum).astype(jnp.bfloat16)


def solution(mesh):
    chips = mesh.devices.reshape(mesh.shape["ctx"] // 2, 2, mesh.shape["tp"])
    split = Mesh(chips, ("yz", "core", "tp"))
    in_specs = (
        P(CTX, "tp"),
        P(CTX, "tp"),
        P(CTX, "tp", None),
        P("tp"),
        P("tp", CTX),
        P("tp"),
        P(CTX, None, None, "tp"),
        P(CTX, "tp", None),
        P(CTX, None),
        P(CTX, None),
    )
    out_specs = P(CTX, "tp")
    return jax.shard_map(body, mesh=split, in_specs=in_specs, out_specs=out_specs, check_vma=False)
```

```python
import jax
import jax.numpy as jnp
from jax import lax
from jax.sharding import Mesh, PartitionSpec as P

WINDOW_KEYS = 128


CTX = ("yz", "core")


def ctx_size():
    return lax.axis_size("yz") * lax.axis_size("core")


def shifted(value, steps):
    count = ctx_size()
    first, last = (max(0, -steps), min(count, count - steps))
    return lax.ppermute(value, CTX, [(source, source + steps) for source in range(first, last)])


def by_core(mine, theirs):
    first = lax.axis_index("core") == 0
    return jnp.stack([jnp.where(first, mine, theirs), jnp.where(first, theirs, mine)], 1)


def other_core(value):
    return lax.ppermute(value, "core", [(0, 1), (1, 0)])


def gathered_columns(block):
    rows = block.T
    spread = jnp.broadcast_to(rows[None], (lax.axis_size("yz"),) + rows.shape)
    mine = lax.all_to_all(spread, "yz", 0, 0, tiled=True)
    return by_core(mine, other_core(mine)).reshape(-1, rows.shape[1])


def to_experts(outbox):
    parts = outbox.reshape((lax.axis_size("yz"), 2) + outbox.shape[1:])
    first = lax.axis_index("core") == 0
    mine = jnp.where(first, parts[:, 0], parts[:, 1])
    theirs = jnp.where(first, parts[:, 1], parts[:, 0])
    staged = by_core(mine, other_core(theirs))
    return lax.all_to_all(staged, "yz", 0, 0, tiled=True).reshape(outbox.shape)


def from_experts(result):
    parts = result.reshape((lax.axis_size("yz"), 2) + result.shape[1:])
    staged = lax.all_to_all(parts, "yz", 0, 0, tiled=True)
    first = lax.axis_index("core") == 0
    mine = jnp.where(first, staged[:, 0], staged[:, 1])
    theirs = jnp.where(first, staged[:, 1], staged[:, 0])
    return by_core(mine, other_core(theirs)).reshape(result.shape)


def attend(query_block, key_blk, value_blk, inside, sink_row_block, factor):
    score = (
        jnp.einsum("rgqd,sgd->gqrs", query_block, key_blk, preferred_element_type=jnp.float32)
        * factor
    )
    masked = jnp.where(inside, score, -1e30)
    top_score = jnp.maximum(jnp.max(masked, -1), sink_row_block[:, :, None])
    expvals = jnp.where(inside, jnp.exp(score - top_score[..., None]), 0.0)
    denominator = jnp.sum(expvals, -1) + jnp.exp(sink_row_block[:, :, None] - top_score)
    probs = (expvals / denominator[..., None]).astype(jnp.bfloat16)
    mixed = jnp.einsum("gqrs,sgd->rgqd", probs, value_blk, preferred_element_type=jnp.float32)
    return mixed.astype(jnp.bfloat16)


def body(
    hidden_in,
    queries,
    rotated_key_value,
    sink_logit_table,
    out_proj,
    norm_gain,
    expert_in,
    expert_out,
    routes,
    route_scores,
):
    tok_rows = hidden_in.shape[0]
    kv_heads = rotated_key_value.shape[1]
    head_dim = rotated_key_value.shape[2] // 2
    q_heads = sink_logit_table.shape[0]
    queries_per_group = q_heads // kv_heads
    factor = head_dim ** (-0.5)
    sink_row_block = sink_logit_table.reshape(kv_heads, queries_per_group)
    earlier = shifted(rotated_key_value, 1)
    keys_all = jnp.concatenate([earlier, rotated_key_value], 0)
    first_pos = lax.axis_index(CTX) * tok_rows
    block_row_count = min(512, tok_rows)
    query_block = queries.reshape(block_row_count, kv_heads, queries_per_group, head_dim)
    query_pos = first_pos + 0 + jnp.arange(block_row_count, dtype=jnp.int32)[:, None]
    key_pos = (
        first_pos
        + 0
        - WINDOW_KEYS
        + jnp.arange(block_row_count + WINDOW_KEYS, dtype=jnp.int32)[None, :]
    )
    inside = (key_pos <= query_pos) & (key_pos > query_pos - WINDOW_KEYS) & (key_pos >= 0)
    mixed = attend(
        query_block,
        keys_all[..., :head_dim],
        keys_all[..., head_dim:],
        inside,
        sink_row_block,
        factor,
    )
    outputs = mixed.reshape(block_row_count, q_heads * head_dim)
    head_partial = lax.dot_general(
        outputs,
        gathered_columns(out_proj),
        (((1,), (1,)), ((), ())),
        preferred_element_type=jnp.float32,
    )
    d_model = head_partial.shape[1]
    tp_count = lax.axis_size("tp")
    tp_index = lax.axis_index("tp")
    quarter_w = d_model // tp_count
    sent = jnp.concatenate([head_partial.astype(jnp.bfloat16), hidden_in], 1)
    assert tp_count == 4
    ahead = [(i, (i + 1) % tp_count) for i in range(tp_count)]
    behind = [(i, (i - 1) % tp_count) for i in range(tp_count)]
    from_behind = lax.ppermute(sent, "tp", ahead)
    from_ahead = lax.ppermute(sent, "tp", behind)
    half_tok = tok_rows // 2
    opposite = jnp.concatenate(
        [
            lax.ppermute(from_behind[:half_tok], "tp", ahead),
            lax.ppermute(from_ahead[half_tok:], "tp", behind),
        ],
        0,
    )
    held = [
        (sent, tp_index),
        (from_behind, (tp_index - 1) % tp_count),
        (from_ahead, (tp_index + 1) % tp_count),
        (opposite, (tp_index + 2) % tp_count),
    ]
    head_sum = held[0][0][:, :d_model].astype(jnp.float32)
    for got, _ in held[1:]:
        head_sum = head_sum + got[:, :d_model].astype(jnp.float32)
    square_total = jnp.zeros((tok_rows,), jnp.float32)
    residual = None
    for got, quarter_id in held:
        part = got[:, d_model:].astype(jnp.float32) + lax.dynamic_slice_in_dim(
            head_sum, quarter_id * quarter_w, quarter_w, 1
        )
        square_total = square_total + jnp.sum(part * part, -1)
        if residual is None:
            residual = part
    normed = (residual * lax.rsqrt(square_total[:, None] / d_model + 1e-05) * norm_gain).astype(
        jnp.bfloat16
    )
    ctx_count = ctx_size()
    top_count = routes.shape[1]
    experts = ctx_count * expert_in.shape[0]
    capacity = max(2, min(tok_rows, 3 * top_count * tok_rows // experts))
    onehot = (routes[:, :, None] == jnp.arange(experts, dtype=jnp.int32)).astype(jnp.int32)
    per_tok = jnp.sum(onehot, 1)
    before = jnp.cumsum(per_tok, axis=0) - per_tok
    slot_ids = jnp.sum(onehot * before[:, None, :], -1)
    flat_index = (routes * capacity + slot_ids).reshape(-1)
    weights = route_scores / jnp.sum(route_scores, -1, keepdims=True)
    spread = jnp.broadcast_to(normed[:, None, :], (tok_rows, top_count, quarter_w)).reshape(
        -1, quarter_w
    )
    outbox = jnp.zeros((experts * capacity, quarter_w), jnp.bfloat16).at[flat_index].set(spread)
    arrived = to_experts(outbox.reshape(ctx_count, capacity, quarter_w)).reshape(-1, quarter_w)
    half_rows = arrived.shape[0] // 2
    from_behind = lax.ppermute(arrived, "tp", ahead)
    from_ahead = lax.ppermute(arrived, "tp", behind)
    first_half = lax.ppermute(from_behind[:half_rows], "tp", ahead)
    second_half = lax.ppermute(from_ahead[half_rows:], "tp", behind)
    opposite = jnp.concatenate([first_half, second_half], 0)
    pieces = [
        (arrived, tp_index),
        (from_behind, (tp_index - 1) % tp_count),
        (from_ahead, (tp_index + 1) % tp_count),
        (opposite, (tp_index + 2) % tp_count),
    ]
    both_vals = None
    for piece, quarter_id in pieces:
        rows = lax.dynamic_slice_in_dim(expert_in[0], quarter_id * quarter_w, quarter_w, 1)
        both_part = jnp.einsum("rk,jkh->jrh", piece, rows, preferred_element_type=jnp.float32)
        both_vals = both_part if both_vals is None else both_vals + both_part
    gate_vals, up_vals = both_vals[0], both_vals[1]
    activated = ((up_vals + 1.0) * gate_vals * jax.nn.sigmoid(1.702 * gate_vals)).astype(
        jnp.bfloat16
    )
    def partial_for(quarter_id):
        cols = lax.dynamic_slice_in_dim(expert_out[0], quarter_id * quarter_w, quarter_w, 1)
        return jnp.dot(activated, cols, preferred_element_type=jnp.float32).astype(jnp.bfloat16)

    across = partial_for((tp_index + 2) % tp_count)
    via_ahead = lax.ppermute(across[:half_rows], "tp", ahead)
    via_behind = lax.ppermute(across[half_rows:], "tp", behind)
    for_ahead = partial_for((tp_index + 1) % tp_count).astype(jnp.float32)
    for_ahead = jnp.concatenate(
        [for_ahead[:half_rows] + via_ahead.astype(jnp.float32), for_ahead[half_rows:]], 0
    ).astype(jnp.bfloat16)
    for_behind = partial_for((tp_index - 1) % tp_count).astype(jnp.float32)
    for_behind = jnp.concatenate(
        [for_behind[:half_rows], for_behind[half_rows:] + via_behind.astype(jnp.float32)], 0
    ).astype(jnp.bfloat16)
    got_behind = lax.ppermute(for_ahead, "tp", ahead)
    got_ahead = lax.ppermute(for_behind, "tp", behind)
    summed = (
        partial_for(tp_index).astype(jnp.float32)
        + got_behind.astype(jnp.float32)
        + got_ahead.astype(jnp.float32)
    )
    result = summed.astype(jnp.bfloat16).reshape(ctx_count, capacity, quarter_w)
    returned = from_experts(result).reshape(-1, quarter_w)
    expert_result = returned[flat_index].reshape(tok_rows, top_count, quarter_w)
    moe_sum = jnp.zeros((tok_rows, quarter_w), jnp.float32)
    for member in range(top_count):
        moe_sum = moe_sum + weights[:, member : member + 1] * expert_result[:, member].astype(
            jnp.float32
        )
    return (residual + moe_sum).astype(jnp.bfloat16)


def solution(mesh):
    chips = mesh.devices.reshape(mesh.shape["ctx"] // 2, 2, mesh.shape["tp"])
    split = Mesh(chips, ("yz", "core", "tp"))
    in_specs = (
        P(CTX, "tp"),
        P(CTX, "tp"),
        P(CTX, "tp", None),
        P("tp"),
        P("tp", CTX),
        P("tp"),
        P(CTX, None, None, "tp"),
        P(CTX, "tp", None),
        P(CTX, None),
        P(CTX, None),
    )
    out_specs = P(CTX, "tp")
    return jax.shard_map(body, mesh=split, in_specs=in_specs, out_specs=out_specs, check_vma=False)
```

```python
import jax
import jax.numpy as jnp
from jax import lax
from jax.sharding import Mesh, PartitionSpec as P

WINDOW_KEYS = 128


CTX = ("yz", "core")


def ctx_size():
    return lax.axis_size("yz") * lax.axis_size("core")


def shifted(value, steps):
    count = ctx_size()
    first, last = (max(0, -steps), min(count, count - steps))
    return lax.ppermute(value, CTX, [(source, source + steps) for source in range(first, last)])


def by_core(mine, theirs):
    first = lax.axis_index("core") == 0
    return jnp.stack([jnp.where(first, mine, theirs), jnp.where(first, theirs, mine)], 1)


def other_core(value):
    return lax.ppermute(value, "core", [(0, 1), (1, 0)])


def gathered_columns(block):
    rows = block.T
    spread = jnp.broadcast_to(rows[None], (lax.axis_size("yz"),) + rows.shape)
    mine = lax.all_to_all(spread, "yz", 0, 0, tiled=True)
    return mine, other_core(mine)


def to_experts(outbox):
    parts = outbox.reshape((lax.axis_size("yz"), 2) + outbox.shape[1:])
    first = lax.axis_index("core") == 0
    mine = jnp.where(first, parts[:, 0], parts[:, 1])
    theirs = jnp.where(first, parts[:, 1], parts[:, 0])
    staged = by_core(mine, other_core(theirs))
    return lax.all_to_all(staged, "yz", 0, 0, tiled=True).reshape(outbox.shape)


def from_experts(result):
    parts = result.reshape((lax.axis_size("yz"), 2) + result.shape[1:])
    staged = lax.all_to_all(parts, "yz", 0, 0, tiled=True)
    first = lax.axis_index("core") == 0
    mine = jnp.where(first, staged[:, 0], staged[:, 1])
    theirs = jnp.where(first, staged[:, 1], staged[:, 0])
    return by_core(mine, other_core(theirs)).reshape(result.shape)


def attend(query_block, key_blk, value_blk, inside, sink_row_block, factor):
    score = (
        jnp.einsum("rgqd,sgd->gqrs", query_block, key_blk, preferred_element_type=jnp.float32)
        * factor
    )
    masked = jnp.where(inside, score, -1e30)
    top_score = jnp.maximum(jnp.max(masked, -1), sink_row_block[:, :, None])
    expvals = jnp.where(inside, jnp.exp(score - top_score[..., None]), 0.0)
    denominator = jnp.sum(expvals, -1) + jnp.exp(sink_row_block[:, :, None] - top_score)
    probs = (expvals / denominator[..., None]).astype(jnp.bfloat16)
    mixed = jnp.einsum("gqrs,sgd->rgqd", probs, value_blk, preferred_element_type=jnp.float32)
    return mixed.astype(jnp.bfloat16)


def body(
    hidden_in,
    queries,
    rotated_key_value,
    sink_logit_table,
    out_proj,
    norm_gain,
    expert_in,
    expert_out,
    routes,
    route_scores,
):
    tok_rows = hidden_in.shape[0]
    kv_heads = rotated_key_value.shape[1]
    head_dim = rotated_key_value.shape[2] // 2
    q_heads = sink_logit_table.shape[0]
    queries_per_group = q_heads // kv_heads
    factor = head_dim ** (-0.5)
    sink_row_block = sink_logit_table.reshape(kv_heads, queries_per_group)
    earlier = shifted(rotated_key_value, 1)
    keys_all = jnp.concatenate([earlier, rotated_key_value], 0)
    first_pos = lax.axis_index(CTX) * tok_rows
    block_row_count = min(512, tok_rows)
    query_block = queries.reshape(block_row_count, kv_heads, queries_per_group, head_dim)
    query_pos = first_pos + 0 + jnp.arange(block_row_count, dtype=jnp.int32)[:, None]
    key_pos = (
        first_pos
        + 0
        - WINDOW_KEYS
        + jnp.arange(block_row_count + WINDOW_KEYS, dtype=jnp.int32)[None, :]
    )
    inside = (key_pos <= query_pos) & (key_pos > query_pos - WINDOW_KEYS) & (key_pos >= 0)
    mixed = attend(
        query_block,
        keys_all[..., :head_dim],
        keys_all[..., head_dim:],
        inside,
        sink_row_block,
        factor,
    )
    outputs = mixed.reshape(block_row_count, q_heads * head_dim)
    own_columns, other_columns = gathered_columns(out_proj)
    contract = (((1,), (2,)), ((), ()))
    own_part = lax.dot_general(outputs, own_columns, contract, preferred_element_type=jnp.float32)
    other_part = lax.dot_general(outputs, other_columns, contract, preferred_element_type=jnp.float32)
    first_core = lax.axis_index("core") == 0
    head_partial = jnp.stack(
        [jnp.where(first_core, own_part, other_part), jnp.where(first_core, other_part, own_part)], 2
    ).reshape(own_part.shape[0], -1)
    d_model = head_partial.shape[1]
    tp_count = lax.axis_size("tp")
    tp_index = lax.axis_index("tp")
    quarter_w = d_model // tp_count
    sent = jnp.concatenate([head_partial.astype(jnp.bfloat16), hidden_in], 1)
    assert tp_count == 4
    ahead = [(i, (i + 1) % tp_count) for i in range(tp_count)]
    behind = [(i, (i - 1) % tp_count) for i in range(tp_count)]
    from_behind = lax.ppermute(sent, "tp", ahead)
    from_ahead = lax.ppermute(sent, "tp", behind)
    half_tok = tok_rows // 2
    opposite = jnp.concatenate(
        [
            lax.ppermute(from_behind[:half_tok], "tp", ahead),
            lax.ppermute(from_ahead[half_tok:], "tp", behind),
        ],
        0,
    )
    held = [
        (sent, tp_index),
        (from_behind, (tp_index - 1) % tp_count),
        (from_ahead, (tp_index + 1) % tp_count),
        (opposite, (tp_index + 2) % tp_count),
    ]
    head_sum = held[0][0][:, :d_model].astype(jnp.float32)
    for got, _ in held[1:]:
        head_sum = head_sum + got[:, :d_model].astype(jnp.float32)
    square_total = jnp.zeros((tok_rows,), jnp.float32)
    residual = None
    for got, quarter_id in held:
        part = got[:, d_model:].astype(jnp.float32) + lax.dynamic_slice_in_dim(
            head_sum, quarter_id * quarter_w, quarter_w, 1
        )
        square_total = square_total + jnp.sum(part * part, -1)
        if residual is None:
            residual = part
    normed = (residual * lax.rsqrt(square_total[:, None] / d_model + 1e-05) * norm_gain).astype(
        jnp.bfloat16
    )
    ctx_count = ctx_size()
    top_count = routes.shape[1]
    experts = ctx_count * expert_in.shape[0]
    capacity = max(2, min(tok_rows, 3 * top_count * tok_rows // experts))
    onehot = (routes[:, :, None] == jnp.arange(experts, dtype=jnp.int32)).astype(jnp.int32)
    per_tok = jnp.sum(onehot, 1)
    before = jnp.cumsum(per_tok, axis=0) - per_tok
    slot_ids = jnp.sum(onehot * before[:, None, :], -1)
    flat_index = (routes * capacity + slot_ids).reshape(-1)
    weights = route_scores / jnp.sum(route_scores, -1, keepdims=True)
    spread = jnp.broadcast_to(normed[:, None, :], (tok_rows, top_count, quarter_w)).reshape(
        -1, quarter_w
    )
    outbox = jnp.zeros((experts * capacity, quarter_w), jnp.bfloat16).at[flat_index].set(spread)
    arrived = to_experts(outbox.reshape(ctx_count, capacity, quarter_w)).reshape(-1, quarter_w)
    half_rows = arrived.shape[0] // 2
    from_behind = lax.ppermute(arrived, "tp", ahead)
    from_ahead = lax.ppermute(arrived, "tp", behind)
    first_half = lax.ppermute(from_behind[:half_rows], "tp", ahead)
    second_half = lax.ppermute(from_ahead[half_rows:], "tp", behind)
    opposite = jnp.concatenate([first_half, second_half], 0)
    pieces = [
        (arrived, tp_index),
        (from_behind, (tp_index - 1) % tp_count),
        (from_ahead, (tp_index + 1) % tp_count),
        (opposite, (tp_index + 2) % tp_count),
    ]
    gate_vals = None
    up_vals = None
    for piece, quarter_id in pieces:
        rows_of = lambda w: lax.dynamic_slice_in_dim(w, quarter_id * quarter_w, quarter_w, 0)
        gate_part = jnp.dot(piece, rows_of(expert_in[0, 0]), preferred_element_type=jnp.float32)
        up_part = jnp.dot(piece, rows_of(expert_in[0, 1]), preferred_element_type=jnp.float32)
        gate_vals = gate_part if gate_vals is None else gate_vals + gate_part
        up_vals = up_part if up_vals is None else up_vals + up_part
    activated = ((up_vals + 1.0) * gate_vals * jax.nn.sigmoid(1.702 * gate_vals)).astype(
        jnp.bfloat16
    )
    def partial_for(quarter_id):
        cols = lax.dynamic_slice_in_dim(expert_out[0], quarter_id * quarter_w, quarter_w, 1)
        return jnp.dot(activated, cols, preferred_element_type=jnp.float32).astype(jnp.bfloat16)

    across = partial_for((tp_index + 2) % tp_count)
    via_ahead = lax.ppermute(across[:half_rows], "tp", ahead)
    via_behind = lax.ppermute(across[half_rows:], "tp", behind)
    for_ahead = partial_for((tp_index + 1) % tp_count).astype(jnp.float32)
    for_ahead = jnp.concatenate(
        [for_ahead[:half_rows] + via_ahead.astype(jnp.float32), for_ahead[half_rows:]], 0
    ).astype(jnp.bfloat16)
    for_behind = partial_for((tp_index - 1) % tp_count).astype(jnp.float32)
    for_behind = jnp.concatenate(
        [for_behind[:half_rows], for_behind[half_rows:] + via_behind.astype(jnp.float32)], 0
    ).astype(jnp.bfloat16)
    got_behind = lax.ppermute(for_ahead, "tp", ahead)
    got_ahead = lax.ppermute(for_behind, "tp", behind)
    summed = (
        partial_for(tp_index).astype(jnp.float32)
        + got_behind.astype(jnp.float32)
        + got_ahead.astype(jnp.float32)
    )
    result = summed.astype(jnp.bfloat16).reshape(ctx_count, capacity, quarter_w)
    returned = lax.all_to_all(result, CTX, 0, 0, tiled=True).reshape(-1, quarter_w)
    expert_result = returned[flat_index].reshape(tok_rows, top_count, quarter_w)
    moe_sum = jnp.zeros((tok_rows, quarter_w), jnp.float32)
    for member in range(top_count):
        moe_sum = moe_sum + weights[:, member : member + 1] * expert_result[:, member].astype(
            jnp.float32
        )
    return (residual + moe_sum).astype(jnp.bfloat16)


def solution(mesh):
    chips = mesh.devices.reshape(mesh.shape["ctx"] // 2, 2, mesh.shape["tp"])
    split = Mesh(chips, ("yz", "core", "tp"))
    in_specs = (
        P(CTX, "tp"),
        P(CTX, "tp"),
        P(CTX, "tp", None),
        P("tp"),
        P("tp", CTX),
        P("tp"),
        P(CTX, None, None, "tp"),
        P(CTX, "tp", None),
        P(CTX, None),
        P(CTX, None),
    )
    out_specs = P(CTX, "tp")
    return jax.shard_map(body, mesh=split, in_specs=in_specs, out_specs=out_specs, check_vma=False)
```

```python
import jax
import jax.numpy as jnp
from jax import lax
from jax.sharding import Mesh, PartitionSpec as P

WINDOW_KEYS = 128


CTX = ("yz", "core")


def ctx_size():
    return lax.axis_size("yz") * lax.axis_size("core")


def shifted(value, steps):
    count = ctx_size()
    first, last = (max(0, -steps), min(count, count - steps))
    return lax.ppermute(value, CTX, [(source, source + steps) for source in range(first, last)])


def by_core(mine, theirs):
    first = lax.axis_index("core") == 0
    return jnp.stack([jnp.where(first, mine, theirs), jnp.where(first, theirs, mine)], 1)


def other_core(value):
    return lax.ppermute(value, "core", [(0, 1), (1, 0)])


def gathered_columns(block):
    rows = block.T
    spread = jnp.broadcast_to(rows[None], (lax.axis_size("yz"),) + rows.shape)
    mine = lax.all_to_all(spread, "yz", 0, 0, tiled=True)
    return by_core(mine, other_core(mine)).reshape(-1, rows.shape[1])


def to_experts(outbox):
    parts = outbox.reshape((lax.axis_size("yz"), 2) + outbox.shape[1:])
    core = lax.axis_index("core")
    mine = lax.dynamic_index_in_dim(parts, core, 1, keepdims=False)
    theirs = lax.dynamic_index_in_dim(parts, 1 - core, 1, keepdims=False)
    staged = by_core(mine, other_core(theirs))
    return lax.all_to_all(staged, "yz", 0, 0, tiled=True).reshape(outbox.shape)


def from_experts(result):
    parts = result.reshape((lax.axis_size("yz"), 2) + result.shape[1:])
    staged = lax.all_to_all(parts, "yz", 0, 0, tiled=True)
    first = lax.axis_index("core") == 0
    mine = jnp.where(first, staged[:, 0], staged[:, 1])
    theirs = jnp.where(first, staged[:, 1], staged[:, 0])
    return by_core(mine, other_core(theirs)).reshape(result.shape)


def attend(query_block, key_blk, value_blk, inside, sink_row_block, factor):
    score = (
        jnp.einsum("rgqd,sgd->gqrs", query_block, key_blk, preferred_element_type=jnp.float32)
        * factor
    )
    masked = jnp.where(inside, score, -1e30)
    top_score = jnp.maximum(jnp.max(masked, -1), sink_row_block[:, :, None])
    expvals = jnp.where(inside, jnp.exp(score - top_score[..., None]), 0.0)
    denominator = jnp.sum(expvals, -1) + jnp.exp(sink_row_block[:, :, None] - top_score)
    probs = (expvals / denominator[..., None]).astype(jnp.bfloat16)
    mixed = jnp.einsum("gqrs,sgd->rgqd", probs, value_blk, preferred_element_type=jnp.float32)
    return mixed.astype(jnp.bfloat16)


def body(
    hidden_in,
    queries,
    rotated_key_value,
    sink_logit_table,
    out_proj,
    norm_gain,
    expert_in,
    expert_out,
    routes,
    route_scores,
):
    tok_rows = hidden_in.shape[0]
    kv_heads = rotated_key_value.shape[1]
    head_dim = rotated_key_value.shape[2] // 2
    q_heads = sink_logit_table.shape[0]
    queries_per_group = q_heads // kv_heads
    factor = head_dim ** (-0.5)
    sink_row_block = sink_logit_table.reshape(kv_heads, queries_per_group)
    earlier = shifted(rotated_key_value, 1)
    keys_all = jnp.concatenate([earlier, rotated_key_value], 0)
    first_pos = lax.axis_index(CTX) * tok_rows
    block_row_count = min(512, tok_rows)
    query_block = queries.reshape(block_row_count, kv_heads, queries_per_group, head_dim)
    query_pos = first_pos + 0 + jnp.arange(block_row_count, dtype=jnp.int32)[:, None]
    key_pos = (
        first_pos
        + 0
        - WINDOW_KEYS
        + jnp.arange(block_row_count + WINDOW_KEYS, dtype=jnp.int32)[None, :]
    )
    inside = (key_pos <= query_pos) & (key_pos > query_pos - WINDOW_KEYS) & (key_pos >= 0)
    mixed = attend(
        query_block,
        keys_all[..., :head_dim],
        keys_all[..., head_dim:],
        inside,
        sink_row_block,
        factor,
    )
    outputs = mixed.reshape(block_row_count, q_heads * head_dim)
    head_partial = lax.dot_general(
        outputs,
        gathered_columns(out_proj),
        (((1,), (1,)), ((), ())),
        preferred_element_type=jnp.float32,
    )
    d_model = head_partial.shape[1]
    tp_count = lax.axis_size("tp")
    tp_index = lax.axis_index("tp")
    quarter_w = d_model // tp_count
    sent = jnp.concatenate([head_partial.astype(jnp.bfloat16), hidden_in], 1)
    assert tp_count == 4
    ahead = [(i, (i + 1) % tp_count) for i in range(tp_count)]
    behind = [(i, (i - 1) % tp_count) for i in range(tp_count)]
    from_behind = lax.ppermute(sent, "tp", ahead)
    from_ahead = lax.ppermute(sent, "tp", behind)
    half_tok = tok_rows // 2
    opposite = jnp.concatenate(
        [
            lax.ppermute(from_behind[:half_tok], "tp", ahead),
            lax.ppermute(from_ahead[half_tok:], "tp", behind),
        ],
        0,
    )
    held = [
        (sent, tp_index),
        (from_behind, (tp_index - 1) % tp_count),
        (from_ahead, (tp_index + 1) % tp_count),
        (opposite, (tp_index + 2) % tp_count),
    ]
    head_sum = held[0][0][:, :d_model].astype(jnp.float32)
    for got, _ in held[1:]:
        head_sum = head_sum + got[:, :d_model].astype(jnp.float32)
    square_total = jnp.zeros((tok_rows,), jnp.float32)
    residual = None
    for got, quarter_id in held:
        part = got[:, d_model:].astype(jnp.float32) + lax.dynamic_slice_in_dim(
            head_sum, quarter_id * quarter_w, quarter_w, 1
        )
        square_total = square_total + jnp.sum(part * part, -1)
        if residual is None:
            residual = part
    normed = (residual * lax.rsqrt(square_total[:, None] / d_model + 1e-05) * norm_gain).astype(
        jnp.bfloat16
    )
    ctx_count = ctx_size()
    top_count = routes.shape[1]
    experts = ctx_count * expert_in.shape[0]
    capacity = max(2, min(tok_rows, 3 * top_count * tok_rows // experts))
    onehot = (routes[:, :, None] == jnp.arange(experts, dtype=jnp.int32)).astype(jnp.int32)
    per_tok = jnp.sum(onehot, 1)
    before = jnp.cumsum(per_tok, axis=0) - per_tok
    slot_ids = jnp.sum(onehot * before[:, None, :], -1)
    flat_index = (routes * capacity + slot_ids).reshape(-1)
    weights = route_scores / jnp.sum(route_scores, -1, keepdims=True)
    spread = jnp.broadcast_to(normed[:, None, :], (tok_rows, top_count, quarter_w)).reshape(
        -1, quarter_w
    )
    outbox = jnp.zeros((experts * capacity, quarter_w), jnp.bfloat16).at[flat_index].set(spread)
    arrived = to_experts(outbox.reshape(ctx_count, capacity, quarter_w)).reshape(-1, quarter_w)
    half_rows = arrived.shape[0] // 2
    from_behind = lax.ppermute(arrived, "tp", ahead)
    from_ahead = lax.ppermute(arrived, "tp", behind)
    first_half = lax.ppermute(from_behind[:half_rows], "tp", ahead)
    second_half = lax.ppermute(from_ahead[half_rows:], "tp", behind)
    opposite = jnp.concatenate([first_half, second_half], 0)
    pieces = [
        (arrived, tp_index),
        (from_behind, (tp_index - 1) % tp_count),
        (from_ahead, (tp_index + 1) % tp_count),
        (opposite, (tp_index + 2) % tp_count),
    ]
    gate_vals = None
    up_vals = None
    for piece, quarter_id in pieces:
        rows_of = lambda w: lax.dynamic_slice_in_dim(w, quarter_id * quarter_w, quarter_w, 0)
        gate_part = jnp.dot(piece, rows_of(expert_in[0, 0]), preferred_element_type=jnp.float32)
        up_part = jnp.dot(piece, rows_of(expert_in[0, 1]), preferred_element_type=jnp.float32)
        gate_vals = gate_part if gate_vals is None else gate_vals + gate_part
        up_vals = up_part if up_vals is None else up_vals + up_part
    activated = ((up_vals + 1.0) * gate_vals * jax.nn.sigmoid(1.702 * gate_vals)).astype(
        jnp.bfloat16
    )
    def partial_for(quarter_id):
        cols = lax.dynamic_slice_in_dim(expert_out[0], quarter_id * quarter_w, quarter_w, 1)
        return jnp.dot(activated, cols, preferred_element_type=jnp.float32).astype(jnp.bfloat16)

    across = partial_for((tp_index + 2) % tp_count)
    via_ahead = lax.ppermute(across[:half_rows], "tp", ahead)
    via_behind = lax.ppermute(across[half_rows:], "tp", behind)
    for_ahead = partial_for((tp_index + 1) % tp_count).astype(jnp.float32)
    for_ahead = jnp.concatenate(
        [for_ahead[:half_rows] + via_ahead.astype(jnp.float32), for_ahead[half_rows:]], 0
    ).astype(jnp.bfloat16)
    for_behind = partial_for((tp_index - 1) % tp_count).astype(jnp.float32)
    for_behind = jnp.concatenate(
        [for_behind[:half_rows], for_behind[half_rows:] + via_behind.astype(jnp.float32)], 0
    ).astype(jnp.bfloat16)
    got_behind = lax.ppermute(for_ahead, "tp", ahead)
    got_ahead = lax.ppermute(for_behind, "tp", behind)
    summed = (
        partial_for(tp_index).astype(jnp.float32)
        + got_behind.astype(jnp.float32)
        + got_ahead.astype(jnp.float32)
    )
    result = summed.astype(jnp.bfloat16).reshape(ctx_count, capacity, quarter_w)
    returned = lax.all_to_all(result, CTX, 0, 0, tiled=True).reshape(-1, quarter_w)
    expert_result = returned[flat_index].reshape(tok_rows, top_count, quarter_w)
    moe_sum = jnp.zeros((tok_rows, quarter_w), jnp.float32)
    for member in range(top_count):
        moe_sum = moe_sum + weights[:, member : member + 1] * expert_result[:, member].astype(
            jnp.float32
        )
    return (residual + moe_sum).astype(jnp.bfloat16)


def solution(mesh):
    chips = mesh.devices.reshape(mesh.shape["ctx"] // 2, 2, mesh.shape["tp"])
    split = Mesh(chips, ("yz", "core", "tp"))
    in_specs = (
        P(CTX, "tp"),
        P(CTX, "tp"),
        P(CTX, "tp", None),
        P("tp"),
        P("tp", CTX),
        P("tp"),
        P(CTX, None, None, "tp"),
        P(CTX, "tp", None),
        P(CTX, None),
        P(CTX, None),
    )
    out_specs = P(CTX, "tp")
    return jax.shard_map(body, mesh=split, in_specs=in_specs, out_specs=out_specs, check_vma=False)
```
